128 devices in a mesh: section: 4 (over z_hi, core), dp: 32 (over x, y, z_lo).
Axes of the slice: x: 4, y: 4, z: 4 (z_hi: 2, z_lo: 2; z = z_hi * 2 + z_lo), core: 2. Of those that a mesh axis runs over, the one named last changes fastest.
Arguments:
- radar_section_input: bfloat16 [2, 32, 128, 2560], P(None, 'dp'), may hold values from -36 to 36
- norm_gain: bfloat16 [4, 2560], P('section'), may hold values from 0.5 to 1.5
- conv_weight: bfloat16 [4, 2240, 2560], P('section', None, 'dp'), may hold values from -0.125 to 0.125
- depth_weight: bfloat16 [4, 7, 2560], P('section'), may hold values from -2 to 2
- out_cotangent: bfloat16 [2, 32, 128, 2560], P(None, 'dp'), may hold values from -6 to 6
Outputs:
- section_outputs: bfloat16 [4, 2, 32, 128, 2560], P('section', None, 'dp')
- input_grads: bfloat16 [4, 2, 32, 128, 2560], P('section', None, 'dp')
- conv_grad: float32 [4, 2240, 2560], P('section', None, 'dp')
- gain_grad: float32 [4, 2560], P('section')
- depth_grad: float32 [4, 7, 2560], P('section')
The draws below stay inside these ranges and needn't reach their ends.
All inputs are finite; a program needn't handle non-finite values.
Results may differ from the reference program's by a relative error of at most 0.033.
Values may be sent and summed in bfloat16 or wider, within the bound.
No kernel may reach another device: no remote copies, remote signals or barrier semaphores. Data moves between devices by JAX's collectives and lax.ppermute only.
A program may use at most 192 MiB of HBM per device.

```python
import math
import jax
import jax.numpy as jnp
from jax import lax

CG = 320
C = 2560
TAPS = 7
KERNEL_TAP_COUNT = 7
DILATION_STEP = 4
MICRO = 2
FRAMES = 128
SECTIONS = 4
SEQS = 32


def draw_radar_section_input(key, part):
    keys = jax.random.split(key, 3)
    shape = (MICRO, SEQS, FRAMES, C)
    base = jnp.clip(jax.random.normal(keys[0], shape, jnp.float32), -4.0, 4.0)
    row_scale = jnp.exp(jax.random.uniform(keys[1], (MICRO, SEQS, FRAMES, 1), jnp.float32, math.log(0.3), math.log(3.0)))
    col_scale = jnp.exp(jax.random.uniform(keys[2], (1, 1, 1, C), jnp.float32, math.log(0.3), math.log(3.0)))
    return (base * row_scale * col_scale).astype(jnp.bfloat16)


def strengthened(result, stream_key, source, target, parts, factor):
    owner, partner = [(jnp.arange(result.shape[axis_at]) // (result.shape[axis_at] // parts)).reshape([-1 if axis == axis_at else 1 for axis in range(result.ndim)]) for axis_at in (source, target)]
    chosen = jax.random.permutation(stream_key, parts)[partner]
    strong = (owner == chosen) | (owner == (partner + parts // 2) % parts)
    return jnp.where(strong, factor * result, result)


def levels(rng, extent, cuts, low, top_value):
    loudness, own = 1.0, jax.random.fold_in(rng, 6)
    for axis_at, parts in cuts:
        draws = jnp.exp(jax.random.uniform(jax.random.fold_in(own, axis_at), (parts,), jnp.float32, low / len(cuts), top_value / len(cuts)))
        loudness = loudness * jnp.repeat(draws, extent[axis_at] // parts).reshape([-1 if axis == axis_at else 1 for axis in range(len(extent))])
    return loudness


def gaussian(rng, extent, deviation, bound, cuts=(), held_as=jnp.bfloat16):
    values = jax.random.normal(rng, extent, jnp.float32) * deviation
    if len(cuts) > 0:
        values = levels(rng, extent, cuts, -0.22, 0.18) * values
    return jnp.clip(values, min=-bound, max=bound).astype(held_as)


def gaussian_with(key, shape, width, bound, shards, heavy, kind=jnp.bfloat16):
    entries = width * jax.random.normal(key, shape, jnp.float32)
    if shards:
        entries = entries * levels(key, shape, shards, -0.22, 0.18)
    return jnp.clip(strengthened(entries, jax.random.fold_in(key, 3), *heavy), -bound, bound).astype(kind)


def setup_inputs(seed: int = 0) -> dict:
    arg_keys = jax.random.split(jax.random.key(seed), 6)
    radar_section_input = draw_radar_section_input(jax.random.fold_in(arg_keys[5], 71), 0)
    norm_gain = jnp.clip(0.5 + 1.0 * jax.random.uniform(arg_keys[1], (SECTIONS, C), jnp.float32) ** levels(arg_keys[1], (SECTIONS, C), ((0, 4),), -0.2, 0.2), 0.5, 1.5).astype(jnp.bfloat16)
    conv_weight = gaussian(arg_keys[2], (SECTIONS, TAPS * CG, C), (TAPS * CG) ** -0.5, 0.125, ((0, 4), (2, 32)))
    depth_weight = gaussian(arg_keys[3], (SECTIONS, KERNEL_TAP_COUNT, C), KERNEL_TAP_COUNT ** -0.5, 2.0, ((0, 4),))
    out_cotangent = gaussian_with(arg_keys[4], (MICRO, SEQS, FRAMES, C), 1.0, 6.0, ((1, 32),), (1, 3, 32, 2.75))
    return dict(radar_section_input=radar_section_input, norm_gain=norm_gain, conv_weight=conv_weight, depth_weight=depth_weight, out_cotangent=out_cotangent)


def shifted(values, offset):
    margin = abs(offset)
    padded = jnp.pad(values, ((margin, margin), (0, 0)))
    return padded[margin + offset:margin + offset + values.shape[0]]

def tap_stack(normed):
    frames, channels = normed.shape
    rows_list = [shifted(normed, tap_index - TAPS // 2) for tap_index in range(TAPS)]
    return jnp.stack(rows_list, 0).reshape(TAPS, frames, channels // CG, CG)

def block_forward(layer_input, gain_row, weight, depth_taps):
    frames, channels = layer_input.shape
    wide_input = layer_input.astype(jnp.float32)
    norm_scale = lax.rsqrt(lax.optimization_barrier(jnp.mean(wide_input * wide_input, axis=-1, keepdims=True)) + 1e-05)
    normed = (wide_input * norm_scale * gain_row.astype(jnp.float32)).astype(jnp.bfloat16)
    tap_weight = weight.reshape(TAPS, CG, channels // CG, CG).astype(jnp.float32)
    conv_out = jnp.einsum('kfgi,kigo->fgo', tap_stack(normed).astype(jnp.float32), tap_weight, precision=lax.Precision.HIGHEST).reshape(frames, channels)
    activated = conv_out * jax.nn.sigmoid(conv_out)
    mixed_out = jnp.zeros_like(activated)
    for delay_index in range(KERNEL_TAP_COUNT):
        delayed_frames = (delay_index - KERNEL_TAP_COUNT // 2) * DILATION_STEP
        mixed_out = mixed_out + shifted(activated, delayed_frames) * depth_taps[delay_index].astype(jnp.float32)
    return ((wide_input + mixed_out).astype(jnp.bfloat16), (norm_scale, normed, conv_out))

def block_backward(layer_input, gain_row, weight, depth_taps, saved_parts, gradient_output):
    norm_scale, normed, conv_out = saved_parts
    frames, channels = layer_input.shape
    grad_wide = gradient_output.astype(jnp.float32)
    sigmoid_gate = jax.nn.sigmoid(conv_out)
    activated = conv_out * sigmoid_gate
    depth_rows = []
    act_grad = jnp.zeros_like(grad_wide)
    for delay_index in range(KERNEL_TAP_COUNT):
        delayed_frames = (delay_index - KERNEL_TAP_COUNT // 2) * DILATION_STEP
        depth_rows.append(lax.optimization_barrier(jnp.sum(grad_wide * shifted(activated, delayed_frames), axis=0)))
        act_grad = act_grad + shifted(grad_wide, -delayed_frames) * depth_taps[delay_index].astype(jnp.float32)
    depth_term = jnp.stack(depth_rows, 0)
    conv_grad_in = (act_grad * sigmoid_gate * (1.0 + conv_out * (1.0 - sigmoid_gate))).astype(jnp.bfloat16)
    gradient_groups = conv_grad_in.reshape(frames, channels // CG, CG).astype(jnp.float32)
    tap_weight = weight.reshape(TAPS, CG, channels // CG, CG).astype(jnp.float32)
    weight_term = jnp.einsum('kfgi,fgo->kigo', tap_stack(normed).astype(jnp.float32), gradient_groups, precision=lax.Precision.HIGHEST).reshape(TAPS * CG, channels)
    per_tap = jnp.einsum('fgo,kigo->kfgi', gradient_groups, tap_weight, precision=lax.Precision.HIGHEST).reshape(TAPS, frames, channels)
    normed_grad = jnp.zeros_like(grad_wide)
    for tap_index in range(TAPS):
        normed_grad = normed_grad + shifted(per_tap[tap_index], TAPS // 2 - tap_index)
    unit_input = layer_input.astype(jnp.float32) * norm_scale
    gain_term = lax.optimization_barrier(jnp.sum(normed_grad * unit_input, axis=0))
    scaled_grad = normed_grad * gain_row.astype(jnp.float32)
    input_grad = (grad_wide + norm_scale * (scaled_grad - unit_input * lax.optimization_barrier(jnp.mean(scaled_grad * unit_input, axis=-1, keepdims=True)))).astype(jnp.bfloat16)
    return (input_grad, weight_term, gain_term, depth_term)

def reference(radar_section_input, norm_gain, conv_weight, depth_weight, out_cotangent):
    inputs = jnp.swapaxes(radar_section_input, 0, 1)
    cotangents = jnp.swapaxes(out_cotangent, 0, 1)
    weight_rows = TAPS * CG

    def one_sequence(totals, sequence_item):
        weight_total, gain_total, depth_total = totals
        seq_inputs, seq_cotangents = sequence_item
        held = [[None] * MICRO for section_index in range(SECTIONS)]
        section_outs = [[None] * MICRO for section_index in range(SECTIONS)]
        for mb_index in range(MICRO):
            current = seq_inputs[mb_index]
            for section_index in range(SECTIONS):
                held[section_index][mb_index] = current
                current, unused_parts = block_forward(current, norm_gain[section_index], conv_weight[section_index], depth_weight[section_index])
                section_outs[section_index][mb_index] = current
        weight_seq = [jnp.zeros((weight_rows, C), jnp.float32) for section_index in range(SECTIONS)]
        gain_seq = [jnp.zeros((C,), jnp.float32) for section_index in range(SECTIONS)]
        depthwise_sequence = [jnp.zeros((KERNEL_TAP_COUNT, C), jnp.float32) for section_index in range(SECTIONS)]
        section_grads = [[None] * MICRO for section_index in range(SECTIONS)]
        for mb_index in range(MICRO):
            gradient_output = seq_cotangents[mb_index]
            for section_index in reversed(range(SECTIONS)):
                layer_input = held[section_index][mb_index]
                saved_parts = block_forward(layer_input, norm_gain[section_index], conv_weight[section_index], depth_weight[section_index])[1]
                gradient_output, weight_term, gain_term, depth_term = block_backward(layer_input, norm_gain[section_index], conv_weight[section_index], depth_weight[section_index], saved_parts, gradient_output)
                section_grads[section_index][mb_index] = gradient_output
                weight_seq[section_index] = weight_seq[section_index] + weight_term
                gain_seq[section_index] = gain_seq[section_index] + gain_term
                depthwise_sequence[section_index] = depthwise_sequence[section_index] + depth_term
        weight_part = jnp.stack(weight_seq, 0)
        rounded = lax.optimization_barrier(weight_part.astype(jnp.bfloat16)).astype(jnp.float32)
        new_totals = (weight_total + rounded, gain_total + jnp.stack(gain_seq, 0), depth_total + jnp.stack(depthwise_sequence, 0))
        outs_block = jnp.stack([jnp.stack(section_outs[section_index], 0) for section_index in range(SECTIONS)], 0)
        grads_block = jnp.stack([jnp.stack(section_grads[section_index], 0) for section_index in range(SECTIONS)], 0)
        return (new_totals, (outs_block, grads_block))
    initial = (jnp.zeros((SECTIONS, weight_rows, C), jnp.float32), jnp.zeros((SECTIONS, C), jnp.float32), jnp.zeros((SECTIONS, KERNEL_TAP_COUNT, C), jnp.float32))
    totals, (outs_all, grads_all) = lax.scan(one_sequence, initial, (inputs, cotangents))
    grad_norm = 1.0 / math.sqrt(MICRO * SEQS * FRAMES)
    section_outputs = jnp.transpose(outs_all, (1, 2, 0, 3, 4))
    input_grads = jnp.transpose(grads_all, (1, 2, 0, 3, 4))
    return (section_outputs, input_grads, totals[0] * grad_norm, totals[1] * grad_norm, totals[2] * grad_norm)
```

```python
import math

import jax
import jax.numpy as jnp
from jax import lax
from jax.sharding import Mesh
from jax.sharding import PartitionSpec as P

CG = 320
TAPS = 7
KERNEL_TAP_COUNT = 7
DILATION_STEP = 4
TIME_AXIS = 2
CHANNELS = 2560


def shift_frames(values, offset):
    if offset == 0:
        return values
    margin = abs(offset)
    frames = values.shape[TIME_AXIS]
    pads = [(0, 0)] * values.ndim
    pads[TIME_AXIS] = (margin, margin)
    padded = jnp.pad(values, pads)
    return lax.slice_in_dim(padded, margin + offset, margin + offset + frames, axis=TIME_AXIS)


def tap_stack(values, sign):
    return jnp.concatenate(
        [shift_frames(values, sign * (tap_index - TAPS // 2)) for tap_index in range(TAPS)], axis=-1
    )


def matmul(left, right):
    lead = left.shape[:-1]
    flat = left.reshape(-1, left.shape[-1])
    out = jnp.dot(flat, right, preferred_element_type=jnp.float32)
    return out.reshape(lead + (right.shape[-1],))


def to_groups(values):
    micro, frames, channels = values.shape
    groups = channels // CG
    parts = values.reshape(micro, frames, groups, CG).transpose(2, 0, 1, 3)
    return lax.all_to_all(parts, "g", 0, 0, tiled=True)


def from_groups(values):
    groups, micro, frames, width = values.shape
    parts = lax.all_to_all(values, "g", 0, 0, tiled=True)
    return parts.transpose(1, 2, 0, 3).reshape(micro, frames, groups * width)


def local(radar_section_input, norm_gain, conv_weight, depth_weight, out_cotangent):
    section_index = lax.axis_index("section")
    section_count = lax.axis_size("section")
    group_index = lax.axis_index("g")
    channels = radar_section_input.shape[3]
    sequences = radar_section_input.shape[1] * lax.axis_size("g") * lax.axis_size("q")
    frames = radar_section_input.shape[2]
    micro_count = radar_section_input.shape[0]

    gain_g = lax.dynamic_slice_in_dim(norm_gain[0], group_index * CG, CG).astype(jnp.float32)
    depth_g = lax.dynamic_slice_in_dim(depth_weight[0], group_index * CG, CG, axis=1).astype(
        jnp.float32
    )
    weight_g = lax.all_gather(conv_weight[0], "q", axis=1, tiled=True)
    weight_back = weight_g.reshape(TAPS, CG, CG).transpose(0, 2, 1).reshape(TAPS * CG, CG)

    radar_g = to_groups(radar_section_input[:, 0])
    cot_g = to_groups(out_cotangent[:, 0])

    zeros_b = jnp.zeros_like(radar_g)
    held_x = zeros_b
    held_normed = zeros_b
    held_out = zeros_b
    held_conv = jnp.zeros(radar_g.shape, jnp.float32)
    held_scale = jnp.zeros(radar_g.shape[:-1] + (1,), jnp.float32)
    arriving = zeros_b
    for step in range(section_count):
        x_in = jnp.where(section_index == 0, radar_g, arriving)
        wide = x_in.astype(jnp.float32)
        sum_sq = lax.psum(jnp.sum(wide * wide, axis=-1, keepdims=True), "g")
        scale = lax.rsqrt(sum_sq * (1.0 / channels) + 1e-05)
        normed = (wide * scale * gain_g).astype(jnp.bfloat16)
        conv_out = matmul(tap_stack(normed, 1), weight_g)
        activated = conv_out * jax.nn.sigmoid(conv_out)
        mixed = jnp.zeros_like(activated)
        for delay_index in range(KERNEL_TAP_COUNT):
            delayed = (delay_index - KERNEL_TAP_COUNT // 2) * DILATION_STEP
            mixed = mixed + shift_frames(activated, delayed) * depth_g[delay_index]
        out = (wide + mixed).astype(jnp.bfloat16)
        keep = section_index == step
        held_x = jnp.where(keep, x_in, held_x)
        held_normed = jnp.where(keep, normed, held_normed)
        held_out = jnp.where(keep, out, held_out)
        held_conv = jnp.where(keep, conv_out, held_conv)
        held_scale = jnp.where(keep, scale, held_scale)
        if step + 1 < section_count:
            arriving = lax.ppermute(
                out, "section", [(s, s + 1) for s in range(section_count - 1)]
            )

    sigmoid_gate = jax.nn.sigmoid(held_conv)
    activated = held_conv * sigmoid_gate
    gate_grad = sigmoid_gate * (1.0 + held_conv * (1.0 - sigmoid_gate))
    unit_input = held_x.astype(jnp.float32) * held_scale
    held_cgi = zeros_b
    held_ig = zeros_b
    acc_depth = jnp.zeros((KERNEL_TAP_COUNT, CG), jnp.float32)
    acc_gain = jnp.zeros((1, CG), jnp.float32)
    incoming = zeros_b
    for step in range(section_count):
        target = section_count - 1 - step
        g_in = jnp.where(section_index == section_count - 1, cot_g, incoming)
        grad_wide = g_in.astype(jnp.float32)
        depth_rows = []
        act_grad = jnp.zeros_like(grad_wide)
        for delay_index in range(KERNEL_TAP_COUNT):
            delayed = (delay_index - KERNEL_TAP_COUNT // 2) * DILATION_STEP
            depth_rows.append(
                jnp.sum(grad_wide * shift_frames(activated, delayed), axis=(0, 1, 2))
            )
            act_grad = act_grad + shift_frames(grad_wide, -delayed) * depth_g[delay_index]
        depth_term = jnp.stack(depth_rows, 0)
        conv_grad_in = (act_grad * gate_grad).astype(jnp.bfloat16)
        normed_grad = matmul(tap_stack(conv_grad_in, -1), weight_back)
        gain_term = jnp.sum(normed_grad * unit_input, axis=(0, 1, 2))[None]
        scaled_grad = normed_grad * gain_g
        mean_term = lax.psum(jnp.sum(scaled_grad * unit_input, axis=-1, keepdims=True), "g")
        input_grad = (
            grad_wide
            + held_scale * (scaled_grad - unit_input * (mean_term * (1.0 / channels)))
        ).astype(jnp.bfloat16)
        keep = section_index == target
        held_cgi = jnp.where(keep, conv_grad_in, held_cgi)
        held_ig = jnp.where(keep, input_grad, held_ig)
        acc_depth = jnp.where(keep, depth_term, acc_depth)
        acc_gain = jnp.where(keep, gain_term, acc_gain)
        if step + 1 < section_count:
            incoming = lax.ppermute(
                input_grad, "section", [(s, s - 1) for s in range(1, section_count)]
            )

    grad_norm = 1.0 / math.sqrt(micro_count * sequences * frames)
    seqs_here = held_normed.shape[0]
    left = tap_stack(held_normed, 1).reshape(seqs_here, micro_count * frames, TAPS * CG)
    right = held_cgi.reshape(seqs_here, micro_count * frames, CG)
    per_seq = jnp.einsum("jrk,jro->jko", left, right, preferred_element_type=jnp.float32)
    weight_part = jnp.sum(per_seq.astype(jnp.bfloat16).astype(jnp.float32), axis=0)
    conv_grad = (
        lax.psum_scatter(weight_part.astype(jnp.bfloat16), "q", scatter_dimension=1, tiled=True)
        .astype(jnp.float32)
        * grad_norm
    )
    small = lax.psum(jnp.concatenate([acc_depth, acc_gain], axis=0), "q")
    small = lax.all_gather(small, "g", axis=1, tiled=True) * grad_norm

    outputs = from_groups(held_out)
    input_grads = from_groups(held_ig)
    return (
        outputs[None, :, None],
        input_grads[None, :, None],
        conv_grad[None],
        small[KERNEL_TAP_COUNT:],
        small[None, :KERNEL_TAP_COUNT],
    )


def solution(mesh):
    sections, dp = mesh.devices.shape
    groups = CHANNELS // CG
    inner = Mesh(mesh.devices.reshape(sections, groups, dp // groups), ("section", "g", "q"))
    dp_axes = ("g", "q")
    return jax.shard_map(
        local,
        mesh=inner,
        in_specs=(
            P(None, dp_axes, None, None),
            P("section", None),
            P("section", None, dp_axes),
            P("section", None, None),
            P(None, dp_axes, None, None),
        ),
        out_specs=(
            P("section", None, dp_axes, None, None),
            P("section", None, dp_axes, None, None),
            P("section", None, dp_axes),
            P("section", None),
            P("section", None, None),
        ),
        check_vma=False,
    )
```

```python
import math

import jax
import jax.numpy as jnp
from jax import lax
from jax.sharding import Mesh
from jax.sharding import PartitionSpec as P

CG = 320
TAPS = 7
KERNEL_TAP_COUNT = 7
DILATION_STEP = 4
TIME_AXIS = 2
CHANNELS = 2560


def shift_frames(values, offset):
    if offset == 0:
        return values
    margin = abs(offset)
    frames = values.shape[TIME_AXIS]
    pads = [(0, 0)] * values.ndim
    pads[TIME_AXIS] = (margin, margin)
    padded = jnp.pad(values, pads)
    return lax.slice_in_dim(padded, margin + offset, margin + offset + frames, axis=TIME_AXIS)


def tap_stack(values, sign):
    return jnp.concatenate(
        [shift_frames(values, sign * (tap_index - TAPS // 2)) for tap_index in range(TAPS)], axis=-1
    )


def matmul(left, right):
    lead = left.shape[:-1]
    flat = left.reshape(-1, left.shape[-1])
    out = jnp.dot(flat, right, preferred_element_type=jnp.float32)
    return out.reshape(lead + (right.shape[-1],))


def to_groups(values):
    micro, frames, channels = values.shape
    groups = channels // CG
    parts = values.reshape(micro, frames, groups, CG).transpose(2, 0, 1, 3)
    return lax.all_to_all(parts, "g", 0, 0, tiled=True)


def from_groups(values):
    groups, micro, frames, width = values.shape
    parts = lax.all_to_all(values, "g", 0, 0, tiled=True)
    return parts.transpose(1, 2, 0, 3).reshape(micro, frames, groups * width)


def sum_over(values, axis):
    count = lax.axis_size(axis)
    bit = 1
    while bit < count:
        values = values + lax.ppermute(values, axis, [(i, i ^ bit) for i in range(count)])
        bit *= 2
    return values


def local(radar_section_input, norm_gain, conv_weight, depth_weight, out_cotangent):
    section_index = lax.axis_index("section")
    section_count = lax.axis_size("section")
    group_index = lax.axis_index("g")
    channels = radar_section_input.shape[3]
    sequences = radar_section_input.shape[1] * lax.axis_size("g") * lax.axis_size("q")
    frames = radar_section_input.shape[2]
    micro_count = radar_section_input.shape[0]

    gain_g = lax.dynamic_slice_in_dim(norm_gain[0], group_index * CG, CG).astype(jnp.float32)
    depth_g = lax.dynamic_slice_in_dim(depth_weight[0], group_index * CG, CG, axis=1).astype(
        jnp.float32
    )
    weight_g = lax.all_gather(conv_weight[0], "q", axis=1, tiled=True)
    weight_back = weight_g.reshape(TAPS, CG, CG).transpose(0, 2, 1).reshape(TAPS * CG, CG)

    radar_g = to_groups(radar_section_input[:, 0])
    cot_g = to_groups(out_cotangent[:, 0])

    zeros_b = jnp.zeros_like(radar_g)
    held_x = zeros_b
    held_normed = zeros_b
    held_out = zeros_b
    held_conv = jnp.zeros(radar_g.shape, jnp.float32)
    held_scale = jnp.zeros(radar_g.shape[:-1] + (1,), jnp.float32)
    arriving = zeros_b
    for step in range(section_count):
        x_in = jnp.where(section_index == 0, radar_g, arriving)
        wide = x_in.astype(jnp.float32)
        sum_sq = sum_over(jnp.sum(wide * wide, axis=-1, keepdims=True), "g")
        scale = lax.rsqrt(sum_sq * (1.0 / channels) + 1e-05)
        normed = (wide * scale * gain_g).astype(jnp.bfloat16)
        conv_out = matmul(tap_stack(normed, 1), weight_g)
        activated = conv_out * jax.nn.sigmoid(conv_out)
        mixed = jnp.zeros_like(activated)
        for delay_index in range(KERNEL_TAP_COUNT):
            delayed = (delay_index - KERNEL_TAP_COUNT // 2) * DILATION_STEP
            mixed = mixed + shift_frames(activated, delayed) * depth_g[delay_index]
        out = (wide + mixed).astype(jnp.bfloat16)
        keep = section_index == step
        held_x = jnp.where(keep, x_in, held_x)
        held_normed = jnp.where(keep, normed, held_normed)
        held_out = jnp.where(keep, out, held_out)
        held_conv = jnp.where(keep, conv_out, held_conv)
        held_scale = jnp.where(keep, scale, held_scale)
        if step + 1 < section_count:
            arriving = lax.ppermute(
                out, "section", [(s, s + 1) for s in range(section_count - 1)]
            )

    sigmoid_gate = jax.nn.sigmoid(held_conv)
    activated = held_conv * sigmoid_gate
    gate_grad = sigmoid_gate * (1.0 + held_conv * (1.0 - sigmoid_gate))
    unit_input = held_x.astype(jnp.float32) * held_scale
    held_cgi = zeros_b
    held_ig = zeros_b
    acc_depth = jnp.zeros((KERNEL_TAP_COUNT, CG), jnp.float32)
    acc_gain = jnp.zeros((1, CG), jnp.float32)
    incoming = zeros_b
    for step in range(section_count):
        target = section_count - 1 - step
        g_in = jnp.where(section_index == section_count - 1, cot_g, incoming)
        grad_wide = g_in.astype(jnp.float32)
        depth_rows = []
        act_grad = jnp.zeros_like(grad_wide)
        for delay_index in range(KERNEL_TAP_COUNT):
            delayed = (delay_index - KERNEL_TAP_COUNT // 2) * DILATION_STEP
            depth_rows.append(
                jnp.sum(grad_wide * shift_frames(activated, delayed), axis=(0, 1, 2))
            )
            act_grad = act_grad + shift_frames(grad_wide, -delayed) * depth_g[delay_index]
        depth_term = jnp.stack(depth_rows, 0)
        conv_grad_in = (act_grad * gate_grad).astype(jnp.bfloat16)
        normed_grad = matmul(tap_stack(conv_grad_in, -1), weight_back)
        gain_term = jnp.sum(normed_grad * unit_input, axis=(0, 1, 2))[None]
        scaled_grad = normed_grad * gain_g
        mean_term = sum_over(jnp.sum(scaled_grad * unit_input, axis=-1, keepdims=True), "g")
        input_grad = (
            grad_wide
            + held_scale * (scaled_grad - unit_input * (mean_term * (1.0 / channels)))
        ).astype(jnp.bfloat16)
        keep = section_index == target
        held_cgi = jnp.where(keep, conv_grad_in, held_cgi)
        held_ig = jnp.where(keep, input_grad, held_ig)
        acc_depth = jnp.where(keep, depth_term, acc_depth)
        acc_gain = jnp.where(keep, gain_term, acc_gain)
        if step + 1 < section_count:
            incoming = lax.ppermute(
                input_grad, "section", [(s, s - 1) for s in range(1, section_count)]
            )

    grad_norm = 1.0 / math.sqrt(micro_count * sequences * frames)
    seqs_here = held_normed.shape[0]
    left = tap_stack(held_normed, 1).reshape(seqs_here, micro_count * frames, TAPS * CG)
    right = held_cgi.reshape(seqs_here, micro_count * frames, CG)
    per_seq = jnp.einsum("jrk,jro->jko", left, right, preferred_element_type=jnp.float32)
    weight_part = jnp.sum(per_seq.astype(jnp.bfloat16).astype(jnp.float32), axis=0)
    conv_grad = (
        lax.psum_scatter(weight_part.astype(jnp.bfloat16), "q", scatter_dimension=1, tiled=True)
        .astype(jnp.float32)
        * grad_norm
    )
    small = lax.psum(jnp.concatenate([acc_depth, acc_gain], axis=0), "q")
    placed = lax.dynamic_update_slice_in_dim(
        jnp.zeros((small.shape[0], channels), jnp.float32), small, group_index * CG, axis=1
    )
    small = sum_over(placed, "g") * grad_norm

    outputs = from_groups(held_out)
    input_grads = from_groups(held_ig)
    return (
        outputs[None, :, None],
        input_grads[None, :, None],
        conv_grad[None],
        small[KERNEL_TAP_COUNT:],
        small[None, :KERNEL_TAP_COUNT],
    )


def solution(mesh):
    sections, dp = mesh.devices.shape
    groups = CHANNELS // CG
    inner = Mesh(mesh.devices.reshape(sections, groups, dp // groups), ("section", "g", "q"))
    dp_axes = ("g", "q")
    return jax.shard_map(
        local,
        mesh=inner,
        in_specs=(
            P(None, dp_axes, None, None),
            P("section", None),
            P("section", None, dp_axes),
            P("section", None, None),
            P(None, dp_axes, None, None),
        ),
        out_specs=(
            P("section", None, dp_axes, None, None),
            P("section", None, dp_axes, None, None),
            P("section", None, dp_axes),
            P("section", None),
            P("section", None, None),
        ),
        check_vma=False,
    )
```

```python
import math

import jax
import jax.numpy as jnp
from jax import lax
from jax.sharding import Mesh
from jax.sharding import PartitionSpec as P

CG = 320
TAPS = 7
KERNEL_TAP_COUNT = 7
DILATION_STEP = 4
TIME_AXIS = 2
CHANNELS = 2560


def shift_frames(values, offset):
    if offset == 0:
        return values
    margin = abs(offset)
    frames = values.shape[TIME_AXIS]
    pads = [(0, 0)] * values.ndim
    pads[TIME_AXIS] = (margin, margin)
    padded = jnp.pad(values, pads)
    return lax.slice_in_dim(padded, margin + offset, margin + offset + frames, axis=TIME_AXIS)


def tap_stack(values, sign):
    return jnp.concatenate(
        [shift_frames(values, sign * (tap_index - TAPS // 2)) for tap_index in range(TAPS)], axis=-1
    )


def matmul(left, right):
    lead = left.shape[:-1]
    flat = left.reshape(-1, left.shape[-1])
    out = jnp.dot(flat, right, preferred_element_type=jnp.float32)
    return out.reshape(lead + (right.shape[-1],))


def to_groups(values):
    micro, frames, channels = values.shape
    groups = channels // CG
    parts = values.reshape(micro, frames, groups, CG).transpose(2, 0, 1, 3)
    return lax.all_to_all(parts, "g", 0, 0, tiled=True)


def from_groups(values):
    groups, micro, frames, width = values.shape
    parts = lax.all_to_all(values, "g", 0, 0, tiled=True)
    return parts.transpose(1, 2, 0, 3).reshape(micro, frames, groups * width)


def sum_over(values, axis):
    count = lax.axis_size(axis)
    bit = 1
    while bit < count:
        values = values + lax.ppermute(values, axis, [(i, i ^ bit) for i in range(count)])
        bit *= 2
    return values


def scatter_over(values, axis):
    count = lax.axis_size(axis)
    index = lax.axis_index(axis)
    bit = count // 2
    while bit >= 1:
        width = values.shape[-1] // 2
        upper = (index // bit) % 2 == 1
        low, high = values[..., :width], values[..., width:]
        keep = jnp.where(upper, high, low)
        give = jnp.where(upper, low, high)
        values = keep + lax.ppermute(give, axis, [(i, i ^ bit) for i in range(count)])
        bit //= 2
    return values


def local(radar_section_input, norm_gain, conv_weight, depth_weight, out_cotangent):
    section_index = lax.axis_index("section")
    section_count = lax.axis_size("section")
    group_index = lax.axis_index("g")
    channels = radar_section_input.shape[3]
    sequences = radar_section_input.shape[1] * lax.axis_size("g") * lax.axis_size("q")
    frames = radar_section_input.shape[2]
    micro_count = radar_section_input.shape[0]

    gain_g = lax.dynamic_slice_in_dim(norm_gain[0], group_index * CG, CG).astype(jnp.float32)
    depth_g = lax.dynamic_slice_in_dim(depth_weight[0], group_index * CG, CG, axis=1).astype(
        jnp.float32
    )
    weight_g = lax.all_gather(conv_weight[0], "q", axis=1, tiled=True)
    weight_back = weight_g.reshape(TAPS, CG, CG).transpose(0, 2, 1).reshape(TAPS * CG, CG)

    radar_g = to_groups(radar_section_input[:, 0])
    cot_g = to_groups(out_cotangent[:, 0])

    zeros_b = jnp.zeros_like(radar_g)
    held_x = zeros_b
    held_normed = zeros_b
    held_out = zeros_b
    held_conv = jnp.zeros(radar_g.shape, jnp.float32)
    held_scale = jnp.zeros(radar_g.shape[:-1] + (1,), jnp.float32)
    radar_wide = radar_g.astype(jnp.float32)
    radar_sq = sum_over(jnp.sum(radar_wide * radar_wide, axis=-1, keepdims=True), "g")
    arriving = zeros_b
    arriving_sq = radar_sq
    for step in range(section_count):
        x_in = jnp.where(section_index == 0, radar_g, arriving)
        wide = x_in.astype(jnp.float32)
        sum_sq = jnp.where(section_index == 0, radar_sq, arriving_sq)
        scale = lax.rsqrt(sum_sq * (1.0 / channels) + 1e-05)
        normed = (wide * scale * gain_g).astype(jnp.bfloat16)
        conv_out = matmul(tap_stack(normed, 1), weight_g)
        activated = conv_out * jax.nn.sigmoid(conv_out)
        mixed = jnp.zeros_like(activated)
        for delay_index in range(KERNEL_TAP_COUNT):
            delayed = (delay_index - KERNEL_TAP_COUNT // 2) * DILATION_STEP
            mixed = mixed + shift_frames(activated, delayed) * depth_g[delay_index]
        out = (wide + mixed).astype(jnp.bfloat16)
        keep = section_index == step
        held_x = jnp.where(keep, x_in, held_x)
        held_normed = jnp.where(keep, normed, held_normed)
        held_out = jnp.where(keep, out, held_out)
        held_conv = jnp.where(keep, conv_out, held_conv)
        held_scale = jnp.where(keep, scale, held_scale)
        if step + 1 < section_count:
            forward_pairs = [(s, s + 1) for s in range(section_count - 1)]
            arriving = lax.ppermute(out, "section", forward_pairs)
            out_wide = out.astype(jnp.float32)
            out_sq = sum_over(jnp.sum(out_wide * out_wide, axis=-1, keepdims=True), "g")
            arriving_sq = lax.ppermute(out_sq, "section", forward_pairs)

    sigmoid_gate = jax.nn.sigmoid(held_conv)
    activated = held_conv * sigmoid_gate
    gate_grad = sigmoid_gate * (1.0 + held_conv * (1.0 - sigmoid_gate))
    unit_input = held_x.astype(jnp.float32) * held_scale
    held_cgi = zeros_b
    held_ig = zeros_b
    acc_depth = jnp.zeros((KERNEL_TAP_COUNT, CG), jnp.float32)
    acc_gain = jnp.zeros((1, CG), jnp.float32)
    incoming = zeros_b
    for step in range(section_count):
        target = section_count - 1 - step
        g_in = jnp.where(section_index == section_count - 1, cot_g, incoming)
        grad_wide = g_in.astype(jnp.float32)
        depth_rows = []
        act_grad = jnp.zeros_like(grad_wide)
        for delay_index in range(KERNEL_TAP_COUNT):
            delayed = (delay_index - KERNEL_TAP_COUNT // 2) * DILATION_STEP
            depth_rows.append(
                jnp.sum(grad_wide * shift_frames(activated, delayed), axis=(0, 1, 2))
            )
            act_grad = act_grad + shift_frames(grad_wide, -delayed) * depth_g[delay_index]
        depth_term = jnp.stack(depth_rows, 0)
        conv_grad_in = (act_grad * gate_grad).astype(jnp.bfloat16)
        normed_grad = matmul(tap_stack(conv_grad_in, -1), weight_back)
        gain_term = jnp.sum(normed_grad * unit_input, axis=(0, 1, 2))[None]
        scaled_grad = normed_grad * gain_g
        mean_term = sum_over(jnp.sum(scaled_grad * unit_input, axis=-1, keepdims=True), "g")
        input_grad = (
            grad_wide
            + held_scale * (scaled_grad - unit_input * (mean_term * (1.0 / channels)))
        ).astype(jnp.bfloat16)
        keep = section_index == target
        held_cgi = jnp.where(keep, conv_grad_in, held_cgi)
        held_ig = jnp.where(keep, input_grad, held_ig)
        acc_depth = jnp.where(keep, depth_term, acc_depth)
        acc_gain = jnp.where(keep, gain_term, acc_gain)
        if step + 1 < section_count:
            incoming = lax.ppermute(
                input_grad, "section", [(s, s - 1) for s in range(1, section_count)]
            )

    grad_norm = 1.0 / math.sqrt(micro_count * sequences * frames)
    seqs_here = held_normed.shape[0]
    left = tap_stack(held_normed, 1).reshape(seqs_here, micro_count * frames, TAPS * CG)
    right = held_cgi.reshape(seqs_here, micro_count * frames, CG)
    per_seq = jnp.einsum("jrk,jro->jko", left, right, preferred_element_type=jnp.float32)
    weight_part = jnp.sum(per_seq.astype(jnp.bfloat16).astype(jnp.float32), axis=0)
    conv_grad = scatter_over(weight_part, "q") * grad_norm
    small = sum_over(jnp.concatenate([acc_depth, acc_gain], axis=0), "q")
    placed = lax.dynamic_update_slice_in_dim(
        jnp.zeros((small.shape[0], channels), jnp.float32), small, group_index * CG, axis=1
    )
    small = sum_over(placed, "g") * grad_norm

    outputs = from_groups(held_out)
    input_grads = from_groups(held_ig)
    return (
        outputs[None, :, None],
        input_grads[None, :, None],
        conv_grad[None],
        small[KERNEL_TAP_COUNT:],
        small[None, :KERNEL_TAP_COUNT],
    )


def solution(mesh):
    sections, dp = mesh.devices.shape
    groups = CHANNELS // CG
    inner = Mesh(mesh.devices.reshape(sections, groups, dp // groups), ("section", "g", "q"))
    dp_axes = ("g", "q")
    return jax.shard_map(
        local,
        mesh=inner,
        in_specs=(
            P(None, dp_axes, None, None),
            P("section", None),
            P("section", None, dp_axes),
            P("section", None, None),
            P(None, dp_axes, None, None),
        ),
        out_specs=(
            P("section", None, dp_axes, None, None),
            P("section", None, dp_axes, None, None),
            P("section", None, dp_axes),
            P("section", None),
            P("section", None, None),
        ),
        check_vma=False,
    )
```

```python
import math

import jax
import jax.numpy as jnp
from jax import lax
from jax.sharding import Mesh
from jax.sharding import PartitionSpec as P

CG = 320
TAPS = 7
KERNEL_TAP_COUNT = 7
DILATION_STEP = 4
TIME_AXIS = 2
CHANNELS = 2560


def shift_frames(values, offset):
    if offset == 0:
        return values
    margin = abs(offset)
    frames = values.shape[TIME_AXIS]
    pads = [(0, 0)] * values.ndim
    pads[TIME_AXIS] = (margin, margin)
    padded = jnp.pad(values, pads)
    return lax.slice_in_dim(padded, margin + offset, margin + offset + frames, axis=TIME_AXIS)


def tap_stack(values, sign):
    return jnp.concatenate(
        [shift_frames(values, sign * (tap_index - TAPS // 2)) for tap_index in range(TAPS)], axis=-1
    )


def matmul(left, right):
    lead = left.shape[:-1]
    flat = left.reshape(-1, left.shape[-1])
    out = jnp.dot(flat, right, preferred_element_type=jnp.float32)
    return out.reshape(lead + (right.shape[-1],))


def to_groups(values):
    micro, frames, channels = values.shape
    groups = channels // CG
    parts = values.reshape(micro, frames, groups, CG).transpose(2, 0, 1, 3)
    return lax.all_to_all(parts, "g", 0, 0, tiled=True)


def from_groups(values):
    groups, micro, frames, width = values.shape
    parts = lax.all_to_all(values, "g", 0, 0, tiled=True)
    return parts.transpose(1, 2, 0, 3).reshape(micro, frames, groups * width)


def sum_over(values, axis):
    count = lax.axis_size(axis)
    bit = 1
    while bit < count:
        values = values + lax.ppermute(values, axis, [(i, i ^ bit) for i in range(count)])
        bit *= 2
    return values


def scatter_over(values, axis):
    count = lax.axis_size(axis)
    index = lax.axis_index(axis)
    bit = count // 2
    while bit >= 1:
        width = values.shape[-1] // 2
        upper = (index // bit) % 2 == 1
        low, high = values[..., :width], values[..., width:]
        keep = jnp.where(upper, high, low)
        give = jnp.where(upper, low, high)
        values = keep + lax.ppermute(give, axis, [(i, i ^ bit) for i in range(count)])
        bit //= 2
    return values


def local(radar_section_input, norm_gain, conv_weight, depth_weight, out_cotangent):
    section_index = lax.axis_index("section")
    section_count = lax.axis_size("section")
    group_index = lax.axis_index("g")
    channels = radar_section_input.shape[3]
    sequences = radar_section_input.shape[1] * lax.axis_size("g") * lax.axis_size("q")
    frames = radar_section_input.shape[2]
    micro_count = radar_section_input.shape[0]

    gain_g = lax.dynamic_slice_in_dim(norm_gain[0], group_index * CG, CG).astype(jnp.float32)
    depth_g = lax.dynamic_slice_in_dim(depth_weight[0], group_index * CG, CG, axis=1).astype(
        jnp.float32
    )
    weight_g = lax.all_gather(conv_weight[0], "q", axis=1, tiled=True)
    weight_back = weight_g.reshape(TAPS, CG, CG).transpose(0, 2, 1).reshape(TAPS * CG, CG)

    radar_g = to_groups(radar_section_input[:, 0])
    cot_g = to_groups(out_cotangent[:, 0])

    zeros_b = jnp.zeros_like(radar_g)
    held_x = zeros_b
    held_normed = zeros_b
    held_out = zeros_b
    held_conv = jnp.zeros(radar_g.shape, jnp.float32)
    held_scale = jnp.zeros(radar_g.shape[:-1] + (1,), jnp.float32)
    radar_wide = radar_g.astype(jnp.float32)
    radar_sq = sum_over(jnp.sum(radar_wide * radar_wide, axis=-1, keepdims=True), "g")
    arriving = zeros_b
    arriving_sq = radar_sq
    for step in range(section_count):
        x_in = jnp.where(section_index == 0, radar_g, arriving)
        wide = x_in.astype(jnp.float32)
        sum_sq = jnp.where(section_index == 0, radar_sq, arriving_sq)
        scale = lax.rsqrt(sum_sq * (1.0 / channels) + 1e-05)
        normed = (wide * scale * gain_g).astype(jnp.bfloat16)
        conv_out = matmul(tap_stack(normed, 1), weight_g)
        activated = conv_out * jax.nn.sigmoid(conv_out)
        mixed = jnp.zeros_like(activated)
        for delay_index in range(KERNEL_TAP_COUNT):
            delayed = (delay_index - KERNEL_TAP_COUNT // 2) * DILATION_STEP
            mixed = mixed + shift_frames(activated, delayed) * depth_g[delay_index]
        out = (wide + mixed).astype(jnp.bfloat16)
        keep = section_index == step
        held_x = jnp.where(keep, x_in, held_x)
        held_normed = jnp.where(keep, normed, held_normed)
        held_out = jnp.where(keep, out, held_out)
        held_conv = jnp.where(keep, conv_out, held_conv)
        held_scale = jnp.where(keep, scale, held_scale)
        if step + 1 < section_count:
            forward_pairs = [(s, s + 1) for s in range(section_count - 1)]
            arriving = lax.ppermute(out, "section", forward_pairs)
            out_wide = out.astype(jnp.float32)
            out_sq = sum_over(jnp.sum(out_wide * out_wide, axis=-1, keepdims=True), "g")
            arriving_sq = lax.ppermute(out_sq, "section", forward_pairs)

    sigmoid_gate = jax.nn.sigmoid(held_conv)
    activated = held_conv * sigmoid_gate
    gate_grad = sigmoid_gate * (1.0 + held_conv * (1.0 - sigmoid_gate))
    unit_input = held_x.astype(jnp.float32) * held_scale
    held_cgi = zeros_b
    held_ig = zeros_b
    held_gin = zeros_b
    held_ngrad = jnp.zeros(radar_g.shape, jnp.float32)
    incoming = zeros_b
    for step in range(section_count):
        target = section_count - 1 - step
        g_in = jnp.where(section_index == section_count - 1, cot_g, incoming)
        grad_wide = g_in.astype(jnp.float32)
        act_grad = jnp.zeros_like(grad_wide)
        for delay_index in range(KERNEL_TAP_COUNT):
            delayed = (delay_index - KERNEL_TAP_COUNT // 2) * DILATION_STEP
            act_grad = act_grad + shift_frames(grad_wide, -delayed) * depth_g[delay_index]
        conv_grad_in = (act_grad * gate_grad).astype(jnp.bfloat16)
        normed_grad = matmul(tap_stack(conv_grad_in, -1), weight_back)
        scaled_grad = normed_grad * gain_g
        mean_term = sum_over(jnp.sum(scaled_grad * unit_input, axis=-1, keepdims=True), "g")
        input_grad = (
            grad_wide
            + held_scale * (scaled_grad - unit_input * (mean_term * (1.0 / channels)))
        ).astype(jnp.bfloat16)
        keep = section_index == target
        held_cgi = jnp.where(keep, conv_grad_in, held_cgi)
        held_ig = jnp.where(keep, input_grad, held_ig)
        held_gin = jnp.where(keep, g_in, held_gin)
        held_ngrad = jnp.where(keep, normed_grad, held_ngrad)
        if step + 1 < section_count:
            incoming = lax.ppermute(
                input_grad, "section", [(s, s - 1) for s in range(1, section_count)]
            )

    grad_wide = held_gin.astype(jnp.float32)
    depth_rows = []
    for delay_index in range(KERNEL_TAP_COUNT):
        delayed = (delay_index - KERNEL_TAP_COUNT // 2) * DILATION_STEP
        depth_rows.append(jnp.sum(grad_wide * shift_frames(activated, delayed), axis=(0, 1, 2)))
    acc_depth = jnp.stack(depth_rows, 0)
    acc_gain = jnp.sum(held_ngrad * unit_input, axis=(0, 1, 2))[None]

    grad_norm = 1.0 / math.sqrt(micro_count * sequences * frames)
    seqs_here = held_normed.shape[0]
    left = tap_stack(held_normed, 1).reshape(seqs_here, micro_count * frames, TAPS * CG)
    right = held_cgi.reshape(seqs_here, micro_count * frames, CG)
    per_seq = jnp.einsum("jrk,jro->jko", left, right, preferred_element_type=jnp.float32)
    weight_part = jnp.sum(per_seq.astype(jnp.bfloat16).astype(jnp.float32), axis=0)
    conv_grad = scatter_over(weight_part, "q") * grad_norm
    small = sum_over(jnp.concatenate([acc_depth, acc_gain], axis=0), "q")
    placed = lax.dynamic_update_slice_in_dim(
        jnp.zeros((small.shape[0], channels), jnp.float32), small, group_index * CG, axis=1
    )
    small = sum_over(placed, "g") * grad_norm

    outputs = from_groups(held_out)
    input_grads = from_groups(held_ig)
    return (
        outputs[None, :, None],
        input_grads[None, :, None],
        conv_grad[None],
        small[KERNEL_TAP_COUNT:],
        small[None, :KERNEL_TAP_COUNT],
    )


def solution(mesh):
    sections, dp = mesh.devices.shape
    groups = CHANNELS // CG
    inner = Mesh(mesh.devices.reshape(sections, groups, dp // groups), ("section", "g", "q"))
    dp_axes = ("g", "q")
    return jax.shard_map(
        local,
        mesh=inner,
        in_specs=(
            P(None, dp_axes, None, None),
            P("section", None),
            P("section", None, dp_axes),
            P("section", None, None),
            P(None, dp_axes, None, None),
        ),
        out_specs=(
            P("section", None, dp_axes, None, None),
            P("section", None, dp_axes, None, None),
            P("section", None, dp_axes),
            P("section", None),
            P("section", None, None),
        ),
        check_vma=False,
    )
```

```python
import math

import jax
import jax.numpy as jnp
from jax import lax
from jax.sharding import Mesh
from jax.sharding import PartitionSpec as P

CG = 320
TAPS = 7
KERNEL_TAP_COUNT = 7
DILATION_STEP = 4
TIME_AXIS = 2
CHANNELS = 2560


def shift_frames(values, offset):
    if offset == 0:
        return values
    margin = abs(offset)
    frames = values.shape[TIME_AXIS]
    pads = [(0, 0)] * values.ndim
    pads[TIME_AXIS] = (margin, margin)
    padded = jnp.pad(values, pads)
    return lax.slice_in_dim(padded, margin + offset, margin + offset + frames, axis=TIME_AXIS)


def tap_stack(values, sign):
    return jnp.concatenate(
        [shift_frames(values, sign * (tap_index - TAPS // 2)) for tap_index in range(TAPS)], axis=-1
    )


def matmul(left, right):
    lead = left.shape[:-1]
    flat = left.reshape(-1, left.shape[-1])
    out = jnp.dot(flat, right, preferred_element_type=jnp.float32)
    return out.reshape(lead + (right.shape[-1],))


def to_groups(values):
    micro, frames, channels = values.shape
    groups = channels // CG
    parts = values.reshape(micro, frames, groups, CG).transpose(2, 0, 1, 3)
    return lax.all_to_all(parts, "g", 0, 0, tiled=True)


def from_groups(values):
    groups, micro, frames, width = values.shape
    parts = lax.all_to_all(values, "g", 0, 0, tiled=True)
    return parts.transpose(1, 2, 0, 3).reshape(micro, frames, groups * width)


def sum_over(values, axis):
    count = lax.axis_size(axis)
    bit = 1
    while bit < count:
        values = values + lax.ppermute(values, axis, [(i, i ^ bit) for i in range(count)])
        bit *= 2
    return values


def scatter_over(values, axis):
    count = lax.axis_size(axis)
    index = lax.axis_index(axis)
    bit = count // 2
    while bit >= 1:
        width = values.shape[-1] // 2
        upper = (index // bit) % 2 == 1
        low, high = values[..., :width], values[..., width:]
        keep = jnp.where(upper, high, low)
        give = jnp.where(upper, low, high)
        values = keep + lax.ppermute(give, axis, [(i, i ^ bit) for i in range(count)])
        bit //= 2
    return values


def local(radar_section_input, norm_gain, conv_weight, depth_weight, out_cotangent):
    section_index = lax.axis_index("section")
    section_count = lax.axis_size("section")
    group_index = lax.axis_index("g")
    channels = radar_section_input.shape[3]
    sequences = radar_section_input.shape[1] * lax.axis_size("g") * lax.axis_size("q")
    frames = radar_section_input.shape[2]
    micro_count = radar_section_input.shape[0]

    gain_g = lax.dynamic_slice_in_dim(norm_gain[0], group_index * CG, CG).astype(jnp.float32)
    depth_g = lax.dynamic_slice_in_dim(depth_weight[0], group_index * CG, CG, axis=1).astype(
        jnp.float32
    )
    weight_g = lax.all_gather(conv_weight[0], "q", axis=1, tiled=True)
    weight_back = weight_g.reshape(TAPS, CG, CG).transpose(0, 2, 1).reshape(TAPS * CG, CG)

    radar_g = to_groups(radar_section_input[:, 0])
    cot_g = to_groups(out_cotangent[:, 0])

    zeros_b = jnp.zeros_like(radar_g)
    held_x = zeros_b
    held_normed = zeros_b
    held_out = zeros_b
    held_conv = jnp.zeros(radar_g.shape, jnp.float32)
    held_scale = jnp.zeros(radar_g.shape[:-1] + (1,), jnp.float32)
    radar_wide = radar_g.astype(jnp.float32)
    radar_sq = sum_over(jnp.sum(radar_wide * radar_wide, axis=-1, keepdims=True), "g")
    arriving = zeros_b
    arriving_sq = radar_sq
    for step in range(section_count):
        x_in = jnp.where(section_index == 0, radar_g, arriving)
        wide = x_in.astype(jnp.float32)
        sum_sq = jnp.where(section_index == 0, radar_sq, arriving_sq)
        scale = lax.rsqrt(sum_sq * (1.0 / channels) + 1e-05)
        normed = (wide * scale * gain_g).astype(jnp.bfloat16)
        conv_out = matmul(tap_stack(normed, 1), weight_g)
        activated = conv_out * jax.nn.sigmoid(conv_out)
        mixed = jnp.zeros_like(activated)
        for delay_index in range(KERNEL_TAP_COUNT):
            delayed = (delay_index - KERNEL_TAP_COUNT // 2) * DILATION_STEP
            mixed = mixed + shift_frames(activated, delayed) * depth_g[delay_index]
        out = (wide + mixed).astype(jnp.bfloat16)
        keep = section_index == step
        held_x = jnp.where(keep, x_in, held_x)
        held_normed = jnp.where(keep, normed, held_normed)
        held_out = jnp.where(keep, out, held_out)
        held_conv = jnp.where(keep, conv_out, held_conv)
        held_scale = jnp.where(keep, scale, held_scale)
        held_x, held_normed, held_out, held_conv, held_scale = lax.optimization_barrier(
            (held_x, held_normed, held_out, held_conv, held_scale)
        )
        if step + 1 < section_count:
            forward_pairs = [(s, s + 1) for s in range(section_count - 1)]
            arriving = lax.ppermute(out, "section", forward_pairs)
            out_wide = out.astype(jnp.float32)
            out_sq = sum_over(jnp.sum(out_wide * out_wide, axis=-1, keepdims=True), "g")
            arriving_sq = lax.ppermute(out_sq, "section", forward_pairs)

    sigmoid_gate = jax.nn.sigmoid(held_conv)
    activated = held_conv * sigmoid_gate
    gate_grad = sigmoid_gate * (1.0 + held_conv * (1.0 - sigmoid_gate))
    unit_input = held_x.astype(jnp.float32) * held_scale
    held_cgi = zeros_b
    held_ig = zeros_b
    held_gin = zeros_b
    held_ngrad = jnp.zeros(radar_g.shape, jnp.float32)
    incoming = zeros_b
    for step in range(section_count):
        target = section_count - 1 - step
        g_in = jnp.where(section_index == section_count - 1, cot_g, incoming)
        grad_wide = g_in.astype(jnp.float32)
        act_grad = jnp.zeros_like(grad_wide)
        for delay_index in range(KERNEL_TAP_COUNT):
            delayed = (delay_index - KERNEL_TAP_COUNT // 2) * DILATION_STEP
            act_grad = act_grad + shift_frames(grad_wide, -delayed) * depth_g[delay_index]
        conv_grad_in = (act_grad * gate_grad).astype(jnp.bfloat16)
        normed_grad = matmul(tap_stack(conv_grad_in, -1), weight_back)
        scaled_grad = normed_grad * gain_g
        mean_term = sum_over(jnp.sum(scaled_grad * unit_input, axis=-1, keepdims=True), "g")
        input_grad = (
            grad_wide
            + held_scale * (scaled_grad - unit_input * (mean_term * (1.0 / channels)))
        ).astype(jnp.bfloat16)
        keep = section_index == target
        held_cgi = jnp.where(keep, conv_grad_in, held_cgi)
        held_ig = jnp.where(keep, input_grad, held_ig)
        held_gin = jnp.where(keep, g_in, held_gin)
        held_ngrad = jnp.where(keep, normed_grad, held_ngrad)
        held_cgi, held_ig, held_gin, held_ngrad = lax.optimization_barrier(
            (held_cgi, held_ig, held_gin, held_ngrad)
        )
        if step + 1 < section_count:
            incoming = lax.ppermute(
                input_grad, "section", [(s, s - 1) for s in range(1, section_count)]
            )

    grad_wide = held_gin.astype(jnp.float32)
    depth_rows = []
    for delay_index in range(KERNEL_TAP_COUNT):
        delayed = (delay_index - KERNEL_TAP_COUNT // 2) * DILATION_STEP
        depth_rows.append(jnp.sum(grad_wide * shift_frames(activated, delayed), axis=(0, 1, 2)))
    acc_depth = jnp.stack(depth_rows, 0)
    acc_gain = jnp.sum(held_ngrad * unit_input, axis=(0, 1, 2))[None]

    grad_norm = 1.0 / math.sqrt(micro_count * sequences * frames)
    per_seq = jnp.einsum(
        "jmtk,jmto->jko", tap_stack(held_normed, 1), held_cgi, preferred_element_type=jnp.float32
    )
    weight_part = jnp.sum(per_seq.astype(jnp.bfloat16).astype(jnp.float32), axis=0)
    conv_grad = scatter_over(weight_part, "q") * grad_norm
    small = sum_over(jnp.concatenate([acc_depth, acc_gain], axis=0), "q")
    placed = lax.dynamic_update_slice_in_dim(
        jnp.zeros((small.shape[0], channels), jnp.float32), small, group_index * CG, axis=1
    )
    small = sum_over(placed, "g") * grad_norm

    outputs = from_groups(held_out)
    input_grads = from_groups(held_ig)
    return (
        outputs[None, :, None],
        input_grads[None, :, None],
        conv_grad[None],
        small[KERNEL_TAP_COUNT:],
        small[None, :KERNEL_TAP_COUNT],
    )


def solution(mesh):
    sections, dp = mesh.devices.shape
    groups = CHANNELS // CG
    inner = Mesh(mesh.devices.reshape(sections, groups, dp // groups), ("section", "g", "q"))
    dp_axes = ("g", "q")
    return jax.shard_map(
        local,
        mesh=inner,
        in_specs=(
            P(None, dp_axes, None, None),
            P("section", None),
            P("section", None, dp_axes),
            P("section", None, None),
            P(None, dp_axes, None, None),
        ),
        out_specs=(
            P("section", None, dp_axes, None, None),
            P("section", None, dp_axes, None, None),
            P("section", None, dp_axes),
            P("section", None),
            P("section", None, None),
        ),
        check_vma=False,
    )
```

```python
import math

import jax
import jax.numpy as jnp
from jax import lax
from jax.sharding import Mesh
from jax.sharding import PartitionSpec as P

CG = 320
TAPS = 7
KERNEL_TAP_COUNT = 7
DILATION_STEP = 4
TIME_AXIS = 2
CHANNELS = 2560


def shift_frames(values, offset):
    if offset == 0:
        return values
    margin = abs(offset)
    frames = values.shape[TIME_AXIS]
    pads = [(0, 0)] * values.ndim
    pads[TIME_AXIS] = (margin, margin)
    padded = jnp.pad(values, pads)
    return lax.slice_in_dim(padded, margin + offset, margin + offset + frames, axis=TIME_AXIS)


def tap_stack(values, sign):
    return jnp.concatenate(
        [shift_frames(values, sign * (tap_index - TAPS // 2)) for tap_index in range(TAPS)], axis=-1
    )


def matmul(left, right):
    lead = left.shape[:-1]
    flat = left.reshape(-1, left.shape[-1])
    out = jnp.dot(flat, right, preferred_element_type=jnp.float32)
    return out.reshape(lead + (right.shape[-1],))


def to_groups(values):
    micro, frames, channels = values.shape
    groups = channels // CG
    parts = values.reshape(micro, frames, groups, CG).transpose(2, 0, 1, 3)
    return lax.all_to_all(parts, "g", 0, 0, tiled=True)


def from_groups(values):
    groups, micro, frames, width = values.shape
    parts = lax.all_to_all(values, "g", 0, 0, tiled=True)
    return parts.transpose(1, 2, 0, 3).reshape(micro, frames, groups * width)


def sum_over(values, axis):
    count = lax.axis_size(axis)
    bit = 1
    while bit < count:
        values = values + lax.ppermute(values, axis, [(i, i ^ bit) for i in range(count)])
        bit *= 2
    return values


def scatter_over(values, axis):
    count = lax.axis_size(axis)
    index = lax.axis_index(axis)
    bit = count // 2
    while bit >= 1:
        width = values.shape[-1] // 2
        upper = (index // bit) % 2 == 1
        low, high = values[..., :width], values[..., width:]
        keep = jnp.where(upper, high, low)
        give = jnp.where(upper, low, high)
        values = keep + lax.ppermute(give, axis, [(i, i ^ bit) for i in range(count)])
        bit //= 2
    return values


def local(radar_section_input, norm_gain, conv_weight, depth_weight, out_cotangent):
    section_index = lax.axis_index("section")
    section_count = lax.axis_size("section")
    group_index = lax.axis_index("g")
    channels = radar_section_input.shape[3]
    sequences = radar_section_input.shape[1] * lax.axis_size("g") * lax.axis_size("q")
    frames = radar_section_input.shape[2]
    micro_count = radar_section_input.shape[0]

    gain_g = lax.dynamic_slice_in_dim(norm_gain[0], group_index * CG, CG).astype(jnp.float32)
    depth_g = lax.dynamic_slice_in_dim(depth_weight[0], group_index * CG, CG, axis=1).astype(
        jnp.float32
    )
    weight_g = lax.all_gather(conv_weight[0], "q", axis=1, tiled=True)
    weight_back = weight_g.reshape(TAPS, CG, CG).transpose(0, 2, 1).reshape(TAPS * CG, CG)

    radar_g = to_groups(radar_section_input[:, 0])
    cot_g = to_groups(out_cotangent[:, 0])

    zeros_b = jnp.zeros_like(radar_g)
    held_x = zeros_b
    held_normed = zeros_b
    held_out = zeros_b
    held_conv = jnp.zeros(radar_g.shape, jnp.float32)
    held_scale = jnp.zeros(radar_g.shape[:-1] + (1,), jnp.float32)
    radar_wide = radar_g.astype(jnp.float32)
    radar_sq = sum_over(jnp.sum(radar_wide * radar_wide, axis=-1, keepdims=True), "g")
    arriving = zeros_b
    arriving_sq = radar_sq
    for step in range(section_count):
        x_in = jnp.where(section_index == 0, radar_g, arriving)
        wide = x_in.astype(jnp.float32)
        sum_sq = jnp.where(section_index == 0, radar_sq, arriving_sq)
        scale = lax.rsqrt(sum_sq * (1.0 / channels) + 1e-05)
        normed = (wide * scale * gain_g).astype(jnp.bfloat16)
        conv_out = matmul(tap_stack(normed, 1), weight_g)
        activated = conv_out * jax.nn.sigmoid(conv_out)
        mixed = jnp.zeros_like(activated)
        for delay_index in range(KERNEL_TAP_COUNT):
            delayed = (delay_index - KERNEL_TAP_COUNT // 2) * DILATION_STEP
            mixed = mixed + shift_frames(activated, delayed) * depth_g[delay_index]
        out = (wide + mixed).astype(jnp.bfloat16)
        keep = section_index == step
        held_x = jnp.where(keep, x_in, held_x)
        held_normed = jnp.where(keep, normed, held_normed)
        held_out = jnp.where(keep, out, held_out)
        held_conv = jnp.where(keep, conv_out, held_conv)
        held_scale = jnp.where(keep, scale, held_scale)
        if step + 1 < section_count:
            forward_pairs = [(s, s + 1) for s in range(section_count - 1)]
            arriving = lax.ppermute(out, "section", forward_pairs)
            out_wide = out.astype(jnp.float32)
            out_sq = sum_over(jnp.sum(out_wide * out_wide, axis=-1, keepdims=True), "g")
            arriving_sq = lax.ppermute(out_sq, "section", forward_pairs)

    sigmoid_gate = jax.nn.sigmoid(held_conv)
    activated = held_conv * sigmoid_gate
    gate_grad = sigmoid_gate * (1.0 + held_conv * (1.0 - sigmoid_gate))
    unit_input = held_x.astype(jnp.float32) * held_scale
    held_cgi = zeros_b
    held_ig = zeros_b
    held_gin = zeros_b
    held_ngrad = jnp.zeros(radar_g.shape, jnp.float32)
    incoming = zeros_b
    for step in range(section_count):
        target = section_count - 1 - step
        g_in = jnp.where(section_index == section_count - 1, cot_g, incoming)
        grad_wide = g_in.astype(jnp.float32)
        act_grad = jnp.zeros_like(grad_wide)
        for delay_index in range(KERNEL_TAP_COUNT):
            delayed = (delay_index - KERNEL_TAP_COUNT // 2) * DILATION_STEP
            act_grad = act_grad + shift_frames(grad_wide, -delayed) * depth_g[delay_index]
        conv_grad_in = (act_grad * gate_grad).astype(jnp.bfloat16)
        normed_grad = matmul(tap_stack(conv_grad_in, -1), weight_back)
        scaled_grad = normed_grad * gain_g
        mean_term = sum_over(jnp.sum(scaled_grad * unit_input, axis=-1, keepdims=True), "g")
        input_grad = (
            grad_wide
            + held_scale * (scaled_grad - unit_input * (mean_term * (1.0 / channels)))
        ).astype(jnp.bfloat16)
        keep = section_index == target
        held_cgi = jnp.where(keep, conv_grad_in, held_cgi)
        held_ig = jnp.where(keep, input_grad, held_ig)
        held_gin = jnp.where(keep, g_in, held_gin)
        held_ngrad = jnp.where(keep, normed_grad, held_ngrad)
        if step + 1 < section_count:
            incoming = lax.ppermute(
                input_grad, "section", [(s, s - 1) for s in range(1, section_count)]
            )

    grad_wide = held_gin.astype(jnp.float32)
    depth_rows = []
    for delay_index in range(KERNEL_TAP_COUNT):
        delayed = (delay_index - KERNEL_TAP_COUNT // 2) * DILATION_STEP
        depth_rows.append(jnp.sum(grad_wide * shift_frames(activated, delayed), axis=(0, 1, 2)))
    acc_depth = jnp.stack(depth_rows, 0)
    acc_gain = jnp.sum(held_ngrad * unit_input, axis=(0, 1, 2))[None]

    grad_norm = 1.0 / math.sqrt(micro_count * sequences * frames)
    per_seq = jnp.einsum(
        "jmtk,jmto->jko", tap_stack(held_normed, 1), held_cgi, preferred_element_type=jnp.float32
    )
    weight_part = jnp.sum(per_seq.astype(jnp.bfloat16).astype(jnp.float32), axis=0)
    conv_grad = scatter_over(weight_part, "q") * grad_norm
    small = sum_over(jnp.concatenate([acc_depth, acc_gain], axis=0), "q")
    placed = lax.dynamic_update_slice_in_dim(
        jnp.zeros((small.shape[0], channels), jnp.float32), small, group_index * CG, axis=1
    )
    small = sum_over(placed, "g") * grad_norm

    outputs = from_groups(held_out)
    input_grads = from_groups(held_ig)
    return (
        outputs[None, :, None],
        input_grads[None, :, None],
        conv_grad[None],
        small[KERNEL_TAP_COUNT:],
        small[None, :KERNEL_TAP_COUNT],
    )


def solution(mesh):
    sections, dp = mesh.devices.shape
    groups = CHANNELS // CG
    inner = Mesh(mesh.devices.reshape(sections, groups, dp // groups), ("section", "g", "q"))
    dp_axes = ("g", "q")
    return jax.shard_map(
        local,
        mesh=inner,
        in_specs=(
            P(None, dp_axes, None, None),
            P("section", None),
            P("section", None, dp_axes),
            P("section", None, None),
            P(None, dp_axes, None, None),
        ),
        out_specs=(
            P("section", None, dp_axes, None, None),
            P("section", None, dp_axes, None, None),
            P("section", None, dp_axes),
            P("section", None),
            P("section", None, None),
        ),
        check_vma=False,
    )
```

```python
import math

import jax
import jax.numpy as jnp
from jax import lax
from jax.sharding import Mesh
from jax.sharding import PartitionSpec as P

CG = 320
TAPS = 7
KERNEL_TAP_COUNT = 7
DILATION_STEP = 4
TIME_AXIS = 2
CHANNELS = 2560


def shift_frames(values, offset):
    if offset == 0:
        return values
    margin = abs(offset)
    frames = values.shape[TIME_AXIS]
    pads = [(0, 0)] * values.ndim
    pads[TIME_AXIS] = (margin, margin)
    padded = jnp.pad(values, pads)
    return lax.slice_in_dim(padded, margin + offset, margin + offset + frames, axis=TIME_AXIS)


def tap_stack(values, sign):
    return jnp.concatenate(
        [shift_frames(values, sign * (tap_index - TAPS // 2)) for tap_index in range(TAPS)], axis=-1
    )


def matmul(left, right):
    lead = left.shape[:-1]
    flat = left.reshape(-1, left.shape[-1])
    out = jnp.dot(flat, right, preferred_element_type=jnp.float32)
    return out.reshape(lead + (right.shape[-1],))


def to_groups(values):
    micro, frames, channels = values.shape
    groups = channels // CG
    parts = values.reshape(micro, frames, groups, CG).transpose(2, 0, 1, 3)
    return lax.all_to_all(parts, "g", 0, 0, tiled=True)


def from_groups(values):
    groups, micro, frames, width = values.shape
    parts = lax.all_to_all(values, "g", 0, 0, tiled=True)
    return parts.transpose(1, 2, 0, 3).reshape(micro, frames, groups * width)


def sum_over(values, axis):
    count = lax.axis_size(axis)
    bit = 1
    while bit < count:
        values = values + lax.ppermute(values, axis, [(i, i ^ bit) for i in range(count)])
        bit *= 2
    return values


def scatter_over(values, axis):
    count = lax.axis_size(axis)
    index = lax.axis_index(axis)
    bit = count // 2
    while bit >= 1:
        width = values.shape[-1] // 2
        upper = (index // bit) % 2 == 1
        low, high = values[..., :width], values[..., width:]
        keep = jnp.where(upper, high, low)
        give = jnp.where(upper, low, high)
        values = keep + lax.ppermute(give, axis, [(i, i ^ bit) for i in range(count)])
        bit //= 2
    return values


def pick_step(steps, index):
    return tuple(
        lax.dynamic_index_in_dim(jnp.stack(field, 0), index, 0, keepdims=False)
        for field in zip(*steps)
    )


def local(radar_section_input, norm_gain, conv_weight, depth_weight, out_cotangent):
    section_index = lax.axis_index("section")
    section_count = lax.axis_size("section")
    group_index = lax.axis_index("g")
    channels = radar_section_input.shape[3]
    sequences = radar_section_input.shape[1] * lax.axis_size("g") * lax.axis_size("q")
    frames = radar_section_input.shape[2]
    micro_count = radar_section_input.shape[0]

    gain_g = lax.dynamic_slice_in_dim(norm_gain[0], group_index * CG, CG).astype(jnp.float32)
    depth_g = lax.dynamic_slice_in_dim(depth_weight[0], group_index * CG, CG, axis=1).astype(
        jnp.float32
    )
    weight_g = lax.all_gather(conv_weight[0], "q", axis=1, tiled=True)
    weight_back = weight_g.reshape(TAPS, CG, CG).transpose(0, 2, 1).reshape(TAPS * CG, CG)

    radar_g = to_groups(radar_section_input[:, 0])
    cot_g = to_groups(out_cotangent[:, 0])

    zeros_b = jnp.zeros_like(radar_g)
    forward_steps = []
    radar_wide = radar_g.astype(jnp.float32)
    radar_sq = sum_over(jnp.sum(radar_wide * radar_wide, axis=-1, keepdims=True), "g")
    arriving = zeros_b
    arriving_sq = radar_sq
    for step in range(section_count):
        x_in = jnp.where(section_index == 0, radar_g, arriving)
        wide = x_in.astype(jnp.float32)
        sum_sq = jnp.where(section_index == 0, radar_sq, arriving_sq)
        scale = lax.rsqrt(sum_sq * (1.0 / channels) + 1e-05)
        normed = (wide * scale * gain_g).astype(jnp.bfloat16)
        conv_out = matmul(tap_stack(normed, 1), weight_g)
        activated = conv_out * jax.nn.sigmoid(conv_out)
        mixed = jnp.zeros_like(activated)
        for delay_index in range(KERNEL_TAP_COUNT):
            delayed = (delay_index - KERNEL_TAP_COUNT // 2) * DILATION_STEP
            mixed = mixed + shift_frames(activated, delayed) * depth_g[delay_index]
        out = (wide + mixed).astype(jnp.bfloat16)
        forward_steps.append((x_in, normed, out, conv_out, scale))
        if step + 1 < section_count:
            forward_pairs = [(s, s + 1) for s in range(section_count - 1)]
            arriving = lax.ppermute(out, "section", forward_pairs)
            out_wide = out.astype(jnp.float32)
            out_sq = sum_over(jnp.sum(out_wide * out_wide, axis=-1, keepdims=True), "g")
            arriving_sq = lax.ppermute(out_sq, "section", forward_pairs)

    held_x, held_normed, held_out, held_conv, held_scale = pick_step(forward_steps, section_index)
    sigmoid_gate = jax.nn.sigmoid(held_conv)
    activated = held_conv * sigmoid_gate
    gate_grad = sigmoid_gate * (1.0 + held_conv * (1.0 - sigmoid_gate))
    unit_input = held_x.astype(jnp.float32) * held_scale
    backward_steps = []
    incoming = zeros_b
    for step in range(section_count):
        g_in = jnp.where(section_index == section_count - 1, cot_g, incoming)
        grad_wide = g_in.astype(jnp.float32)
        act_grad = jnp.zeros_like(grad_wide)
        for delay_index in range(KERNEL_TAP_COUNT):
            delayed = (delay_index - KERNEL_TAP_COUNT // 2) * DILATION_STEP
            act_grad = act_grad + shift_frames(grad_wide, -delayed) * depth_g[delay_index]
        conv_grad_in = (act_grad * gate_grad).astype(jnp.bfloat16)
        normed_grad = matmul(tap_stack(conv_grad_in, -1), weight_back)
        scaled_grad = normed_grad * gain_g
        mean_term = sum_over(jnp.sum(scaled_grad * unit_input, axis=-1, keepdims=True), "g")
        input_grad = (
            grad_wide
            + held_scale * (scaled_grad - unit_input * (mean_term * (1.0 / channels)))
        ).astype(jnp.bfloat16)
        backward_steps.append((conv_grad_in, input_grad, g_in, normed_grad))
        if step + 1 < section_count:
            incoming = lax.ppermute(
                input_grad, "section", [(s, s - 1) for s in range(1, section_count)]
            )

    held_cgi, held_ig, held_gin, held_ngrad = pick_step(
        backward_steps, section_count - 1 - section_index
    )
    grad_wide = held_gin.astype(jnp.float32)
    depth_rows = []
    for delay_index in range(KERNEL_TAP_COUNT):
        delayed = (delay_index - KERNEL_TAP_COUNT // 2) * DILATION_STEP
        depth_rows.append(jnp.sum(grad_wide * shift_frames(activated, delayed), axis=(0, 1, 2)))
    acc_depth = jnp.stack(depth_rows, 0)
    acc_gain = jnp.sum(held_ngrad * unit_input, axis=(0, 1, 2))[None]

    grad_norm = 1.0 / math.sqrt(micro_count * sequences * frames)
    per_seq = jnp.einsum(
        "jmtk,jmto->jko", tap_stack(held_normed, 1), held_cgi, preferred_element_type=jnp.float32
    )
    weight_part = jnp.sum(per_seq.astype(jnp.bfloat16).astype(jnp.float32), axis=0)
    conv_grad = scatter_over(weight_part, "q") * grad_norm
    small = sum_over(jnp.concatenate([acc_depth, acc_gain], axis=0), "q")
    placed = lax.dynamic_update_slice_in_dim(
        jnp.zeros((small.shape[0], channels), jnp.float32), small, group_index * CG, axis=1
    )
    small = sum_over(placed, "g") * grad_norm

    outputs = from_groups(held_out)
    input_grads = from_groups(held_ig)
    return (
        outputs[None, :, None],
        input_grads[None, :, None],
        conv_grad[None],
        small[KERNEL_TAP_COUNT:],
        small[None, :KERNEL_TAP_COUNT],
    )


def solution(mesh):
    sections, dp = mesh.devices.shape
    groups = CHANNELS // CG
    inner = Mesh(mesh.devices.reshape(sections, groups, dp // groups), ("section", "g", "q"))
    dp_axes = ("g", "q")
    return jax.shard_map(
        local,
        mesh=inner,
        in_specs=(
            P(None, dp_axes, None, None),
            P("section", None),
            P("section", None, dp_axes),
            P("section", None, None),
            P(None, dp_axes, None, None),
        ),
        out_specs=(
            P("section", None, dp_axes, None, None),
            P("section", None, dp_axes, None, None),
            P("section", None, dp_axes),
            P("section", None),
            P("section", None, None),
        ),
        check_vma=False,
    )
```

```python
import math

import jax
import jax.numpy as jnp
from jax import lax
from jax.sharding import Mesh
from jax.sharding import PartitionSpec as P

CG = 320
TAPS = 7
KERNEL_TAP_COUNT = 7
DILATION_STEP = 4
TIME_AXIS = 2
CHANNELS = 2560


def shift_frames(values, offset):
    if offset == 0:
        return values
    margin = abs(offset)
    frames = values.shape[TIME_AXIS]
    pads = [(0, 0)] * values.ndim
    pads[TIME_AXIS] = (margin, margin)
    padded = jnp.pad(values, pads)
    return lax.slice_in_dim(padded, margin + offset, margin + offset + frames, axis=TIME_AXIS)


def tap_stack(values, sign):
    return jnp.concatenate(
        [shift_frames(values, sign * (tap_index - TAPS // 2)) for tap_index in range(TAPS)], axis=-1
    )


def matmul(left, right):
    lead = left.shape[:-1]
    flat = left.reshape(-1, left.shape[-1])
    out = jnp.dot(flat, right, preferred_element_type=jnp.float32)
    return out.reshape(lead + (right.shape[-1],))


def to_groups(values):
    micro, frames, channels = values.shape
    groups = channels // CG
    parts = values.reshape(micro, frames, groups, CG).transpose(2, 0, 1, 3)
    return lax.all_to_all(parts, "g", 0, 0, tiled=True)


def from_groups(values):
    groups, micro, frames, width = values.shape
    parts = lax.all_to_all(values, "g", 0, 0, tiled=True)
    return parts.transpose(1, 2, 0, 3).reshape(micro, frames, groups * width)


def sum_over(values, axis):
    count = lax.axis_size(axis)
    bit = 1
    while bit < count:
        values = values + lax.ppermute(values, axis, [(i, i ^ bit) for i in range(count)])
        bit *= 2
    return values


def scatter_over(values, axis):
    count = lax.axis_size(axis)
    index = lax.axis_index(axis)
    bit = count // 2
    while bit >= 1:
        width = values.shape[-1] // 2
        upper = (index // bit) % 2 == 1
        low, high = values[..., :width], values[..., width:]
        keep = jnp.where(upper, high, low)
        give = jnp.where(upper, low, high)
        values = keep + lax.ppermute(give, axis, [(i, i ^ bit) for i in range(count)])
        bit //= 2
    return values


def local(radar_section_input, norm_gain, conv_weight, depth_weight, out_cotangent):
    section_index = lax.axis_index("section")
    section_count = lax.axis_size("section")
    group_index = lax.axis_index("g")
    channels = radar_section_input.shape[3]
    sequences = radar_section_input.shape[1] * lax.axis_size("g") * lax.axis_size("q")
    frames = radar_section_input.shape[2]
    micro_count = radar_section_input.shape[0]

    gain_g = lax.dynamic_slice_in_dim(norm_gain[0], group_index * CG, CG).astype(jnp.float32)
    depth_g = lax.dynamic_slice_in_dim(depth_weight[0], group_index * CG, CG, axis=1).astype(
        jnp.float32
    )
    weight_g = lax.all_gather(conv_weight[0], "q", axis=1, tiled=True)
    weight_back = weight_g.reshape(TAPS, CG, CG).transpose(0, 2, 1).reshape(TAPS * CG, CG)

    radar_g = to_groups(radar_section_input[:, 0])
    cot_g = to_groups(out_cotangent[:, 0])

    zeros_b = jnp.zeros_like(radar_g)
    held_x = zeros_b
    held_normed = zeros_b
    held_out = zeros_b
    held_conv = jnp.zeros(radar_g.shape, jnp.float32)
    held_scale = jnp.zeros(radar_g.shape[:-1] + (1,), jnp.float32)
    radar_wide = radar_g.astype(jnp.float32)
    radar_sq = sum_over(jnp.sum(radar_wide * radar_wide, axis=-1, keepdims=True), "g")
    arriving = zeros_b
    arriving_sq = radar_sq
    for step in range(section_count):
        x_in = jnp.where(section_index == 0, radar_g, arriving)
        wide = x_in.astype(jnp.float32)
        sum_sq = jnp.where(section_index == 0, radar_sq, arriving_sq)
        scale = lax.rsqrt(sum_sq * (1.0 / channels) + 1e-05)
        normed = (wide * scale * gain_g).astype(jnp.bfloat16)
        conv_out = matmul(tap_stack(normed, 1), weight_g)
        activated = conv_out * jax.nn.sigmoid(conv_out)
        mixed = jnp.zeros_like(activated)
        for delay_index in range(KERNEL_TAP_COUNT):
            delayed = (delay_index - KERNEL_TAP_COUNT // 2) * DILATION_STEP
            mixed = mixed + shift_frames(activated, delayed) * depth_g[delay_index]
        out = (wide + mixed).astype(jnp.bfloat16)
        keep = section_index == step
        held_x = jnp.where(keep, x_in, held_x)
        held_normed = jnp.where(keep, normed, held_normed)
        held_out = jnp.where(keep, out, held_out)
        held_conv = jnp.where(keep, conv_out, held_conv)
        held_scale = jnp.where(keep, scale, held_scale)
        if step + 1 < section_count:
            forward_pairs = [(step, step + 1)]
            arriving = lax.ppermute(out, "section", forward_pairs)
            out_wide = out.astype(jnp.float32)
            out_sq = sum_over(jnp.sum(out_wide * out_wide, axis=-1, keepdims=True), "g")
            arriving_sq = lax.ppermute(out_sq, "section", forward_pairs)

    sigmoid_gate = jax.nn.sigmoid(held_conv)
    activated = held_conv * sigmoid_gate
    gate_grad = sigmoid_gate * (1.0 + held_conv * (1.0 - sigmoid_gate))
    unit_input = held_x.astype(jnp.float32) * held_scale
    held_cgi = zeros_b
    held_ig = zeros_b
    held_gin = zeros_b
    held_ngrad = jnp.zeros(radar_g.shape, jnp.float32)
    incoming = zeros_b
    for step in range(section_count):
        target = section_count - 1 - step
        g_in = jnp.where(section_index == section_count - 1, cot_g, incoming)
        grad_wide = g_in.astype(jnp.float32)
        act_grad = jnp.zeros_like(grad_wide)
        for delay_index in range(KERNEL_TAP_COUNT):
            delayed = (delay_index - KERNEL_TAP_COUNT // 2) * DILATION_STEP
            act_grad = act_grad + shift_frames(grad_wide, -delayed) * depth_g[delay_index]
        conv_grad_in = (act_grad * gate_grad).astype(jnp.bfloat16)
        normed_grad = matmul(tap_stack(conv_grad_in, -1), weight_back)
        scaled_grad = normed_grad * gain_g
        mean_term = sum_over(jnp.sum(scaled_grad * unit_input, axis=-1, keepdims=True), "g")
        input_grad = (
            grad_wide
            + held_scale * (scaled_grad - unit_input * (mean_term * (1.0 / channels)))
        ).astype(jnp.bfloat16)
        keep = section_index == target
        held_cgi = jnp.where(keep, conv_grad_in, held_cgi)
        held_ig = jnp.where(keep, input_grad, held_ig)
        held_gin = jnp.where(keep, g_in, held_gin)
        held_ngrad = jnp.where(keep, normed_grad, held_ngrad)
        if step + 1 < section_count:
            incoming = lax.ppermute(input_grad, "section", [(target, target - 1)])

    grad_wide = held_gin.astype(jnp.float32)
    depth_rows = []
    for delay_index in range(KERNEL_TAP_COUNT):
        delayed = (delay_index - KERNEL_TAP_COUNT // 2) * DILATION_STEP
        depth_rows.append(jnp.sum(grad_wide * shift_frames(activated, delayed), axis=(0, 1, 2)))
    acc_depth = jnp.stack(depth_rows, 0)
    acc_gain = jnp.sum(held_ngrad * unit_input, axis=(0, 1, 2))[None]

    grad_norm = 1.0 / math.sqrt(micro_count * sequences * frames)
    per_seq = jnp.einsum(
        "jmtk,jmto->jko", tap_stack(held_normed, 1), held_cgi, preferred_element_type=jnp.float32
    )
    weight_part = jnp.sum(per_seq.astype(jnp.bfloat16).astype(jnp.float32), axis=0)
    conv_grad = scatter_over(weight_part, "q") * grad_norm
    small = sum_over(jnp.concatenate([acc_depth, acc_gain], axis=0), "q")
    placed = lax.dynamic_update_slice_in_dim(
        jnp.zeros((small.shape[0], channels), jnp.float32), small, group_index * CG, axis=1
    )
    small = sum_over(placed, "g") * grad_norm

    outputs = from_groups(held_out)
    input_grads = from_groups(held_ig)
    return (
        outputs[None, :, None],
        input_grads[None, :, None],
        conv_grad[None],
        small[KERNEL_TAP_COUNT:],
        small[None, :KERNEL_TAP_COUNT],
    )


def solution(mesh):
    sections, dp = mesh.devices.shape
    groups = CHANNELS // CG
    inner = Mesh(mesh.devices.reshape(sections, groups, dp // groups), ("section", "g", "q"))
    dp_axes = ("g", "q")
    return jax.shard_map(
        local,
        mesh=inner,
        in_specs=(
            P(None, dp_axes, None, None),
            P("section", None),
            P("section", None, dp_axes),
            P("section", None, None),
            P(None, dp_axes, None, None),
        ),
        out_specs=(
            P("section", None, dp_axes, None, None),
            P("section", None, dp_axes, None, None),
            P("section", None, dp_axes),
            P("section", None),
            P("section", None, None),
        ),
        check_vma=False,
    )
```

```python
import math

import jax
import jax.numpy as jnp
from jax import lax
from jax.sharding import Mesh
from jax.sharding import PartitionSpec as P

CG = 320
TAPS = 7
KERNEL_TAP_COUNT = 7
DILATION_STEP = 4
TIME_AXIS = 2
CHANNELS = 2560


def shift_frames(values, offset):
    if offset == 0:
        return values
    margin = abs(offset)
    frames = values.shape[TIME_AXIS]
    pads = [(0, 0)] * values.ndim
    pads[TIME_AXIS] = (margin, margin)
    padded = jnp.pad(values, pads)
    return lax.slice_in_dim(padded, margin + offset, margin + offset + frames, axis=TIME_AXIS)


def tap_stack(values, sign):
    return jnp.concatenate(
        [shift_frames(values, sign * (tap_index - TAPS // 2)) for tap_index in range(TAPS)], axis=-1
    )


def matmul(left, right):
    lead = left.shape[:-1]
    flat = left.reshape(-1, left.shape[-1])
    out = jnp.dot(flat, right, preferred_element_type=jnp.float32)
    return out.reshape(lead + (right.shape[-1],))


def to_groups(values):
    micro, frames, channels = values.shape
    groups = channels // CG
    parts = values.reshape(micro, frames, groups, CG).transpose(2, 0, 1, 3)
    return lax.all_to_all(parts, "g", 0, 0, tiled=True)


def from_groups(values):
    groups, micro, frames, width = values.shape
    parts = lax.all_to_all(values, "g", 0, 0, tiled=True)
    return parts.transpose(1, 2, 0, 3).reshape(micro, frames, groups * width)


def sum_over(values, axis):
    count = lax.axis_size(axis)
    bit = 1
    while bit < count:
        values = values + lax.ppermute(values, axis, [(i, i ^ bit) for i in range(count)])
        bit *= 2
    return values


def scatter_over(values, axis):
    count = lax.axis_size(axis)
    index = lax.axis_index(axis)
    bit = count // 2
    while bit >= 1:
        width = values.shape[-1] // 2
        upper = (index // bit) % 2 == 1
        low, high = values[..., :width], values[..., width:]
        keep = jnp.where(upper, high, low)
        give = jnp.where(upper, low, high)
        sent = lax.ppermute(give.astype(jnp.bfloat16), axis, [(i, i ^ bit) for i in range(count)])
        values = keep + sent.astype(jnp.float32)
        bit //= 2
    return values


def local(radar_section_input, norm_gain, conv_weight, depth_weight, out_cotangent):
    section_index = lax.axis_index("section")
    section_count = lax.axis_size("section")
    group_index = lax.axis_index("g")
    channels = radar_section_input.shape[3]
    sequences = radar_section_input.shape[1] * lax.axis_size("g") * lax.axis_size("q")
    frames = radar_section_input.shape[2]
    micro_count = radar_section_input.shape[0]

    gain_g = lax.dynamic_slice_in_dim(norm_gain[0], group_index * CG, CG).astype(jnp.float32)
    depth_g = lax.dynamic_slice_in_dim(depth_weight[0], group_index * CG, CG, axis=1).astype(
        jnp.float32
    )
    weight_g = lax.all_gather(conv_weight[0], "q", axis=1, tiled=True)
    weight_back = weight_g.reshape(TAPS, CG, CG).transpose(0, 2, 1).reshape(TAPS * CG, CG)

    radar_g = to_groups(radar_section_input[:, 0])
    cot_g = to_groups(out_cotangent[:, 0])

    zeros_b = jnp.zeros_like(radar_g)
    held_x = zeros_b
    held_normed = zeros_b
    held_out = zeros_b
    held_conv = jnp.zeros(radar_g.shape, jnp.float32)
    held_scale = jnp.zeros(radar_g.shape[:-1] + (1,), jnp.float32)
    radar_wide = radar_g.astype(jnp.float32)
    radar_sq = sum_over(jnp.sum(radar_wide * radar_wide, axis=-1, keepdims=True), "g")
    arriving = zeros_b
    arriving_sq = radar_sq
    for step in range(section_count):
        x_in = jnp.where(section_index == 0, radar_g, arriving)
        wide = x_in.astype(jnp.float32)
        sum_sq = jnp.where(section_index == 0, radar_sq, arriving_sq)
        scale = lax.rsqrt(sum_sq * (1.0 / channels) + 1e-05)
        normed = (wide * scale * gain_g).astype(jnp.bfloat16)
        conv_out = matmul(tap_stack(normed, 1), weight_g)
        activated = conv_out * jax.nn.sigmoid(conv_out)
        mixed = jnp.zeros_like(activated)
        for delay_index in range(KERNEL_TAP_COUNT):
            delayed = (delay_index - KERNEL_TAP_COUNT // 2) * DILATION_STEP
            mixed = mixed + shift_frames(activated, delayed) * depth_g[delay_index]
        out = (wide + mixed).astype(jnp.bfloat16)
        keep = section_index == step
        held_x = jnp.where(keep, x_in, held_x)
        held_normed = jnp.where(keep, normed, held_normed)
        held_out = jnp.where(keep, out, held_out)
        held_conv = jnp.where(keep, conv_out, held_conv)
        held_scale = jnp.where(keep, scale, held_scale)
        if step + 1 < section_count:
            forward_pairs = [(step, step + 1)]
            arriving = lax.ppermute(out, "section", forward_pairs)
            out_wide = out.astype(jnp.float32)
            out_sq = sum_over(jnp.sum(out_wide * out_wide, axis=-1, keepdims=True), "g")
            arriving_sq = lax.ppermute(out_sq, "section", forward_pairs)

    sigmoid_gate = jax.nn.sigmoid(held_conv)
    activated = held_conv * sigmoid_gate
    gate_grad = sigmoid_gate * (1.0 + held_conv * (1.0 - sigmoid_gate))
    unit_input = held_x.astype(jnp.float32) * held_scale
    held_cgi = zeros_b
    held_ig = zeros_b
    held_gin = zeros_b
    held_ngrad = jnp.zeros(radar_g.shape, jnp.float32)
    incoming = zeros_b
    for step in range(section_count):
        target = section_count - 1 - step
        g_in = jnp.where(section_index == section_count - 1, cot_g, incoming)
        grad_wide = g_in.astype(jnp.float32)
        act_grad = jnp.zeros_like(grad_wide)
        for delay_index in range(KERNEL_TAP_COUNT):
            delayed = (delay_index - KERNEL_TAP_COUNT // 2) * DILATION_STEP
            act_grad = act_grad + shift_frames(grad_wide, -delayed) * depth_g[delay_index]
        conv_grad_in = (act_grad * gate_grad).astype(jnp.bfloat16)
        normed_grad = matmul(tap_stack(conv_grad_in, -1), weight_back)
        scaled_grad = normed_grad * gain_g
        mean_term = sum_over(jnp.sum(scaled_grad * unit_input, axis=-1, keepdims=True), "g")
        input_grad = (
            grad_wide
            + held_scale * (scaled_grad - unit_input * (mean_term * (1.0 / channels)))
        ).astype(jnp.bfloat16)
        keep = section_index == target
        held_cgi = jnp.where(keep, conv_grad_in, held_cgi)
        held_ig = jnp.where(keep, input_grad, held_ig)
        held_gin = jnp.where(keep, g_in, held_gin)
        held_ngrad = jnp.where(keep, normed_grad, held_ngrad)
        if step + 1 < section_count:
            incoming = lax.ppermute(input_grad, "section", [(target, target - 1)])

    grad_wide = held_gin.astype(jnp.float32)
    depth_rows = []
    for delay_index in range(KERNEL_TAP_COUNT):
        delayed = (delay_index - KERNEL_TAP_COUNT // 2) * DILATION_STEP
        depth_rows.append(jnp.sum(grad_wide * shift_frames(activated, delayed), axis=(0, 1, 2)))
    acc_depth = jnp.stack(depth_rows, 0)
    acc_gain = jnp.sum(held_ngrad * unit_input, axis=(0, 1, 2))[None]

    grad_norm = 1.0 / math.sqrt(micro_count * sequences * frames)
    per_seq = jnp.einsum(
        "jmtk,jmto->jko", tap_stack(held_normed, 1), held_cgi, preferred_element_type=jnp.float32
    )
    weight_part = jnp.sum(per_seq.astype(jnp.bfloat16).astype(jnp.float32), axis=0)
    conv_grad = scatter_over(weight_part, "q") * grad_norm
    small = sum_over(jnp.concatenate([acc_depth, acc_gain], axis=0), "q")
    placed = lax.dynamic_update_slice_in_dim(
        jnp.zeros((small.shape[0], channels), jnp.float32), small, group_index * CG, axis=1
    )
    small = sum_over(placed, "g") * grad_norm

    outputs = from_groups(held_out)
    input_grads = from_groups(held_ig)
    return (
        outputs[None, :, None],
        input_grads[None, :, None],
        conv_grad[None],
        small[KERNEL_TAP_COUNT:],
        small[None, :KERNEL_TAP_COUNT],
    )


def solution(mesh):
    sections, dp = mesh.devices.shape
    groups = CHANNELS // CG
    inner = Mesh(mesh.devices.reshape(sections, groups, dp // groups), ("section", "g", "q"))
    dp_axes = ("g", "q")
    return jax.shard_map(
        local,
        mesh=inner,
        in_specs=(
            P(None, dp_axes, None, None),
            P("section", None),
            P("section", None, dp_axes),
            P("section", None, None),
            P(None, dp_axes, None, None),
        ),
        out_specs=(
            P("section", None, dp_axes, None, None),
            P("section", None, dp_axes, None, None),
            P("section", None, dp_axes),
            P("section", None),
            P("section", None, None),
        ),
        check_vma=False,
    )
```

```python
import math

import jax
import jax.numpy as jnp
from jax import lax
from jax.sharding import Mesh
from jax.sharding import PartitionSpec as P

CG = 320
TAPS = 7
KERNEL_TAP_COUNT = 7
DILATION_STEP = 4
TIME_AXIS = 2
CHANNELS = 2560


def shift_frames(values, offset):
    if offset == 0:
        return values
    margin = abs(offset)
    frames = values.shape[TIME_AXIS]
    pads = [(0, 0)] * values.ndim
    pads[TIME_AXIS] = (margin, margin)
    padded = jnp.pad(values, pads)
    return lax.slice_in_dim(padded, margin + offset, margin + offset + frames, axis=TIME_AXIS)


def tap_stack(values, sign):
    return jnp.concatenate(
        [shift_frames(values, sign * (tap_index - TAPS // 2)) for tap_index in range(TAPS)], axis=-1
    )


def matmul(left, right):
    lead = left.shape[:-1]
    flat = left.reshape(-1, left.shape[-1])
    out = jnp.dot(flat, right, preferred_element_type=jnp.float32)
    return out.reshape(lead + (right.shape[-1],))


def to_groups(values):
    micro, frames, channels = values.shape
    groups = channels // CG
    parts = values.reshape(micro, frames, groups, CG).transpose(2, 0, 1, 3)
    return lax.all_to_all(parts, "g", 0, 0, tiled=True)


def from_groups(values):
    groups, micro, frames, width = values.shape
    parts = lax.all_to_all(values, "g", 0, 0, tiled=True)
    return parts.transpose(1, 2, 0, 3).reshape(micro, frames, groups * width)


def sum_over(values, axis):
    count = lax.axis_size(axis)
    bit = 1
    while bit < count:
        values = values + lax.ppermute(values, axis, [(i, i ^ bit) for i in range(count)])
        bit *= 2
    return values


def scatter_over(values, axis):
    count = lax.axis_size(axis)
    index = lax.axis_index(axis)
    bit = count // 2
    while bit >= 1:
        width = values.shape[-1] // 2
        upper = (index // bit) % 2 == 1
        low, high = values[..., :width], values[..., width:]
        keep = jnp.where(upper, high, low)
        give = jnp.where(upper, low, high)
        sent = lax.ppermute(give.astype(jnp.bfloat16), axis, [(i, i ^ bit) for i in range(count)])
        values = keep + sent.astype(jnp.float32)
        bit //= 2
    return values


def local(radar_section_input, norm_gain, conv_weight, depth_weight, out_cotangent):
    section_index = lax.axis_index("section")
    section_count = lax.axis_size("section")
    group_index = lax.axis_index("g")
    channels = radar_section_input.shape[3]
    sequences = radar_section_input.shape[1] * lax.axis_size("g") * lax.axis_size("q")
    frames = radar_section_input.shape[2]
    micro_count = radar_section_input.shape[0]

    gain_g = lax.dynamic_slice_in_dim(norm_gain[0], group_index * CG, CG).astype(jnp.float32)
    depth_g = lax.dynamic_slice_in_dim(depth_weight[0], group_index * CG, CG, axis=1).astype(
        jnp.float32
    )
    weight_g = lax.all_gather(conv_weight[0], "q", axis=1, tiled=True)
    weight_back = weight_g.reshape(TAPS, CG, CG).transpose(0, 2, 1).reshape(TAPS * CG, CG)

    radar_g = to_groups(radar_section_input[:, 0])
    cot_g = to_groups(out_cotangent[:, 0])

    zeros_b = jnp.zeros_like(radar_g)
    held_x = zeros_b
    held_normed = zeros_b
    held_out = zeros_b
    held_conv = jnp.zeros(radar_g.shape, jnp.float32)
    held_scale = jnp.zeros(radar_g.shape[:-1] + (1,), jnp.float32)
    own_wide = radar_section_input[:, 0].astype(jnp.float32)
    own_sq = jnp.sum(own_wide * own_wide, axis=-1, keepdims=True)
    group_count = lax.axis_size("g")
    radar_sq = lax.all_to_all(
        jnp.broadcast_to(own_sq[None], (group_count,) + own_sq.shape), "g", 0, 0, tiled=True
    )
    arriving = zeros_b
    arriving_sq = radar_sq
    for step in range(section_count):
        x_in = jnp.where(section_index == 0, radar_g, arriving)
        wide = x_in.astype(jnp.float32)
        sum_sq = jnp.where(section_index == 0, radar_sq, arriving_sq)
        scale = lax.rsqrt(sum_sq * (1.0 / channels) + 1e-05)
        normed = (wide * scale * gain_g).astype(jnp.bfloat16)
        conv_out = matmul(tap_stack(normed, 1), weight_g)
        activated = conv_out * jax.nn.sigmoid(conv_out)
        mixed = jnp.zeros_like(activated)
        for delay_index in range(KERNEL_TAP_COUNT):
            delayed = (delay_index - KERNEL_TAP_COUNT // 2) * DILATION_STEP
            mixed = mixed + shift_frames(activated, delayed) * depth_g[delay_index]
        out = (wide + mixed).astype(jnp.bfloat16)
        keep = section_index == step
        held_x = jnp.where(keep, x_in, held_x)
        held_normed = jnp.where(keep, normed, held_normed)
        held_out = jnp.where(keep, out, held_out)
        held_conv = jnp.where(keep, conv_out, held_conv)
        held_scale = jnp.where(keep, scale, held_scale)
        if step + 1 < section_count:
            forward_pairs = [(step, step + 1)]
            arriving = lax.ppermute(out, "section", forward_pairs)
            out_wide = out.astype(jnp.float32)
            out_sq = sum_over(jnp.sum(out_wide * out_wide, axis=-1, keepdims=True), "g")
            arriving_sq = lax.ppermute(out_sq, "section", forward_pairs)

    sigmoid_gate = jax.nn.sigmoid(held_conv)
    activated = held_conv * sigmoid_gate
    gate_grad = sigmoid_gate * (1.0 + held_conv * (1.0 - sigmoid_gate))
    unit_input = held_x.astype(jnp.float32) * held_scale
    held_cgi = zeros_b
    held_ig = zeros_b
    held_gin = zeros_b
    held_ngrad = jnp.zeros(radar_g.shape, jnp.float32)
    incoming = zeros_b
    for step in range(section_count):
        target = section_count - 1 - step
        g_in = jnp.where(section_index == section_count - 1, cot_g, incoming)
        grad_wide = g_in.astype(jnp.float32)
        act_grad = jnp.zeros_like(grad_wide)
        for delay_index in range(KERNEL_TAP_COUNT):
            delayed = (delay_index - KERNEL_TAP_COUNT // 2) * DILATION_STEP
            act_grad = act_grad + shift_frames(grad_wide, -delayed) * depth_g[delay_index]
        conv_grad_in = (act_grad * gate_grad).astype(jnp.bfloat16)
        normed_grad = matmul(tap_stack(conv_grad_in, -1), weight_back)
        scaled_grad = normed_grad * gain_g
        mean_term = sum_over(jnp.sum(scaled_grad * unit_input, axis=-1, keepdims=True), "g")
        input_grad = (
            grad_wide
            + held_scale * (scaled_grad - unit_input * (mean_term * (1.0 / channels)))
        ).astype(jnp.bfloat16)
        keep = section_index == target
        held_cgi = jnp.where(keep, conv_grad_in, held_cgi)
        held_ig = jnp.where(keep, input_grad, held_ig)
        held_gin = jnp.where(keep, g_in, held_gin)
        held_ngrad = jnp.where(keep, normed_grad, held_ngrad)
        if step + 1 < section_count:
            incoming = lax.ppermute(input_grad, "section", [(target, target - 1)])

    grad_wide = held_gin.astype(jnp.float32)
    depth_rows = []
    for delay_index in range(KERNEL_TAP_COUNT):
        delayed = (delay_index - KERNEL_TAP_COUNT // 2) * DILATION_STEP
        depth_rows.append(jnp.sum(grad_wide * shift_frames(activated, delayed), axis=(0, 1, 2)))
    acc_depth = jnp.stack(depth_rows, 0)
    acc_gain = jnp.sum(held_ngrad * unit_input, axis=(0, 1, 2))[None]

    grad_norm = 1.0 / math.sqrt(micro_count * sequences * frames)
    per_seq = jnp.einsum(
        "jmtk,jmto->jko", tap_stack(held_normed, 1), held_cgi, preferred_element_type=jnp.float32
    )
    weight_part = jnp.sum(per_seq.astype(jnp.bfloat16).astype(jnp.float32), axis=0)
    conv_grad = scatter_over(weight_part, "q") * grad_norm
    small = sum_over(jnp.concatenate([acc_depth, acc_gain], axis=0), "q")
    placed = lax.dynamic_update_slice_in_dim(
        jnp.zeros((small.shape[0], channels), jnp.float32), small, group_index * CG, axis=1
    )
    small = sum_over(placed, "g") * grad_norm

    outputs = from_groups(held_out)
    input_grads = from_groups(held_ig)
    return (
        outputs[None, :, None],
        input_grads[None, :, None],
        conv_grad[None],
        small[KERNEL_TAP_COUNT:],
        small[None, :KERNEL_TAP_COUNT],
    )


def solution(mesh):
    sections, dp = mesh.devices.shape
    groups = CHANNELS // CG
    inner = Mesh(mesh.devices.reshape(sections, groups, dp // groups), ("section", "g", "q"))
    dp_axes = ("g", "q")
    return jax.shard_map(
        local,
        mesh=inner,
        in_specs=(
            P(None, dp_axes, None, None),
            P("section", None),
            P("section", None, dp_axes),
            P("section", None, None),
            P(None, dp_axes, None, None),
        ),
        out_specs=(
            P("section", None, dp_axes, None, None),
            P("section", None, dp_axes, None, None),
            P("section", None, dp_axes),
            P("section", None),
            P("section", None, None),
        ),
        check_vma=False,
    )
```
